32 devices in a mesh: gx: 4 (over y, core), gy: 8 (over z, x).
Axes of the slice: x: 2, y: 2, z: 4, core: 2. Of those that a mesh axis runs over, the one named last changes fastest.
Arguments:
- control: float32 [3, 256, 1024], P(None, 'gy', 'gx'), may hold values from -2 to 2
- perts: float32 [16, 3, 256, 1024], P(None, None, 'gy', 'gx'), may hold values from -2.8 to 2.8
Outputs:
- basis: float32 [16, 3, 256, 1024], P(None, None, 'gy', 'gx')
- rfactor: float32 [16, 16], replicated
The draws below stay inside these ranges and needn't reach their ends.
All inputs are finite; a program needn't handle non-finite values.
Results may differ from the reference program's by a relative error of at most 0.0003.
Values sent between devices are 32-bit elements; how exact they have to be, the bound alone decides.
No kernel may reach another device: no remote copies, remote signals or barrier semaphores. Data moves between devices by JAX's collectives and lax.ppermute only.
A program may use at most 64 MiB of HBM per device.

```python
import math
import jax
import jax.numpy as jnp
from jax import lax

MEMBERS = 16
STEPS = 2
NY = 256
NX = 1024


def draw_perts(key, part):
    keys = jax.random.split(jax.random.fold_in(key, 17), 4)
    exponent = jax.random.uniform(keys[3], (MEMBERS, 1, 1, 1), jnp.float32, 0.0, 1.0)
    scales = 0.05 * jnp.power(10.0, exponent)
    weight_matrix = jax.random.uniform(keys[2], (MEMBERS, 1, 1, 1), jnp.float32, -1.0, 1.0)
    noise = jnp.clip(jax.random.normal(keys[0], (MEMBERS, 3, NY, NX), jnp.float32), -4.0, 4.0)
    common = jnp.clip(jax.random.normal(keys[1], (1, 3, NY, NX), jnp.float32), -4.0, 4.0)
    field = 0.6 * noise + 0.8 * weight_matrix * common
    return (scales * field).astype(jnp.float32)


def steps_of(stream_key, shape, pieces, least, largest):
    def one(axis_at, blocks):
        steps = jax.random.uniform(jax.random.fold_in(jax.random.fold_in(stream_key, 6), axis_at), (blocks,), jnp.float32, least / len(pieces), largest / len(pieces))
        return jnp.repeat(jnp.exp(steps), shape[axis_at] // blocks).reshape((-1,) + (1,) * (len(shape) - axis_at - 1))

    gain = one(*pieces[0])
    for cut in pieces[1:]:
        gain = gain * one(*cut)
    return gain


def centred(rng, dims, deviation, reach, shards=(), kind=jnp.bfloat16):
    array = jax.random.normal(rng, dims, jnp.float32) * deviation
    if len(shards) > 0:
        array = steps_of(rng, dims, shards, -0.22, 0.18) * array
    return jnp.clip(array, min=-reach, max=reach).astype(kind)


def setup_inputs(seed: int = 0) -> dict:
    streams_of = jax.random.split(jax.random.key(seed), 3)
    return {
        "control": centred(streams_of[0], (3, NY, NX), 0.5, 2.0, ((1, 8), (2, 4)), jnp.float32),
        "perts": draw_perts(jax.random.fold_in(streams_of[2], 71), 0),
    }


mean_depth = 4.0
gravity = 1.0
coriolis_mid = 0.5
time_step = 0.1
two_pi = 2.0 * math.pi

def slope_x(field):
    return (8.0 * (jnp.roll(field, -1, -1) - jnp.roll(field, 1, -1)) - (jnp.roll(field, -2, -1) - jnp.roll(field, 2, -1))) / 12.0

def slope_y(field):
    return (8.0 * (jnp.roll(field, -1, -2) - jnp.roll(field, 1, -2)) - (jnp.roll(field, -2, -2) - jnp.roll(field, 2, -2))) / 12.0

def tendency(model_state, coriolis_parameter):
    height, east_wind, north_wind = (model_state[0], model_state[1], model_state[2])
    depth = mean_depth + height
    change_h = -(slope_x(depth * east_wind) + slope_y(depth * north_wind))
    change_e = -(east_wind * slope_x(east_wind) + north_wind * slope_y(east_wind)) + coriolis_parameter * north_wind - gravity * slope_x(height)
    change_n = -(east_wind * slope_x(north_wind) + north_wind * slope_y(north_wind)) - coriolis_parameter * east_wind - gravity * slope_y(height)
    return jnp.stack([change_h, change_e, change_n], 0)

def prediction_state(model_state, coriolis_parameter):
    for step in range(STEPS):
        first = tendency(model_state, coriolis_parameter)
        middle = model_state + time_step * first
        second = tendency(middle, coriolis_parameter)
        model_state = model_state + 0.5 * time_step * (first + second)
    return model_state

def reference(control, perts):
    rows = jnp.arange(NY).astype(jnp.float32)
    coriolis_parameter = (coriolis_mid * (1.0 + 0.5 * jnp.sin(two_pi * rows / float(NY))))[:, None]
    control_prediction = prediction_state(control, coriolis_parameter)

    def member(perturbation_field):
        return prediction_state(control + perturbation_field, coriolis_parameter) - control_prediction
    bred = lax.map(member, perts)
    flat = bred.reshape(MEMBERS, -1)
    gram = jnp.dot(flat, flat.T, precision=lax.Precision.HIGHEST)
    lower = jnp.linalg.cholesky(gram)
    solved = jax.scipy.linalg.solve_triangular(lower, flat, lower=True)
    domain_length = 3 * NY * NX
    basis = (math.sqrt(domain_length) * solved).reshape(perts.shape)
    rfactor = lower.T / math.sqrt(domain_length)
    return (basis, rfactor)
```

```python
import math

import jax
import jax.numpy as jnp
from jax import lax
from jax.sharding import PartitionSpec as P

MEMBERS = 16
STEPS = 2


mean_depth = 4.0
gravity = 1.0
coriolis_mid = 0.5
time_step = 0.1
two_pi = 2.0 * math.pi


def with_halo(value, sides, width):
    for axis, dim in sides:
        count, length = (lax.axis_size(axis), value.shape[dim])
        up = [(i, (i + 1) % count) for i in range(count)]
        down = [(j, i) for i, j in up]
        last = lax.slice_in_dim(value, length - width, length, axis=dim)
        initial = lax.slice_in_dim(value, 0, width, axis=dim)
        before = lax.ppermute(last, axis, up)
        after = lax.ppermute(initial, axis, down)
        value = jnp.concatenate([before, value, after], axis=dim)
    return value


def slope_x(padded):
    inner = padded[..., 2:-2, :]
    return (8.0 * (inner[..., 3:-1] - inner[..., 1:-3]) - (inner[..., 4:] - inner[..., :-4])) / 12.0


def slope_y(padded):
    inner = padded[..., :, 2:-2]
    return (
        8.0 * (inner[..., 3:-1, :] - inner[..., 1:-3, :]) - (inner[..., 4:, :] - inner[..., :-4, :])
    ) / 12.0


def center(padded):
    return padded[..., 2:-2, 2:-2]


def tendency(padded, coriolis_parameter):
    wide_h, wide_e, wide_n = (padded[..., 0, :, :], padded[..., 1, :, :], padded[..., 2, :, :])
    east_wind, north_wind = (center(wide_e), center(wide_n))
    depth = mean_depth + wide_h
    change_h = -(slope_x(depth * wide_e) + slope_y(depth * wide_n))
    change_e = (
        -(east_wind * slope_x(wide_e) + north_wind * slope_y(wide_e))
        + coriolis_parameter * north_wind
        - gravity * slope_x(wide_h)
    )
    change_n = (
        -(east_wind * slope_x(wide_n) + north_wind * slope_y(wide_n))
        - coriolis_parameter * east_wind
        - gravity * slope_y(wide_h)
    )
    return jnp.stack([change_h, change_e, change_n], -3)


def body(control, perts):
    tile_rows, tile_column_count = (control.shape[1], control.shape[2])
    grid_rows = tile_rows * lax.axis_size("gy")
    grid_cols = tile_column_count * lax.axis_size("gx")
    first_row = lax.axis_index("gy") * tile_rows

    def coriolis_rows(margin):
        rows = (first_row - margin + jnp.arange(tile_rows + 2 * margin, dtype=jnp.int32)).astype(
            jnp.float32
        )
        return (coriolis_mid * (1.0 + 0.5 * jnp.sin(two_pi * rows / float(grid_rows))))[:, None]

    states = jnp.concatenate([control[None], control[None] + perts], 0)
    margin = 4 * STEPS
    current = with_halo(states, (("gx", 3), ("gy", 2)), margin)
    for step in range(STEPS):
        first = tendency(current, coriolis_rows(margin - 2))
        middle = current[..., 2:-2, 2:-2] + time_step * first
        second = tendency(middle, coriolis_rows(margin - 4))
        current = current[..., 4:-4, 4:-4] + 0.5 * time_step * (first[..., 2:-2, 2:-2] + second)
        margin = margin - 4
    bred = current[1:] - current[0:1]
    flat = bred.reshape(MEMBERS, -1)
    local_gram = jnp.dot(flat, flat.T, precision=lax.Precision.HIGHEST)
    gram = local_gram
    for axis in ("gx", "gy"):
        count = lax.axis_size(axis)
        if count & (count - 1):
            gram = lax.psum(gram, axis)
            continue
        stride = 1
        while stride < count:
            pairs = [(i, i ^ stride) for i in range(count)]
            gram = gram + lax.ppermute(gram, axis, pairs)
            stride *= 2
    lower = jnp.linalg.cholesky(gram)
    solved = jax.scipy.linalg.solve_triangular(lower, flat, lower=True)
    domain_length = 3 * grid_rows * grid_cols
    basis = (math.sqrt(domain_length) * solved).reshape(perts.shape)
    rfactor = lower.T / math.sqrt(domain_length)
    return (basis, rfactor)


def solution(mesh):
    in_specs = (P(None, "gy", "gx"), P(None, None, "gy", "gx"))
    out_specs = (P(None, None, "gy", "gx"), P())
    return jax.shard_map(body, mesh=mesh, in_specs=in_specs, out_specs=out_specs, check_vma=False)
```

```python
import math

import jax
import jax.numpy as jnp
from jax import lax
from jax.sharding import PartitionSpec as P

MEMBERS = 16
STEPS = 2


mean_depth = 4.0
gravity = 1.0
coriolis_mid = 0.5
time_step = 0.1
two_pi = 2.0 * math.pi


def with_halo(value, width):
    rows, cols = (value.shape[-2], value.shape[-1])
    across, down = (lax.axis_size("gx"), lax.axis_size("gy"))

    def shift(part, axes, dx, dy):
        pairs = []
        for x in range(across):
            for y in range(down):
                target = ((x + dx) % across, (y + dy) % down)
                if axes == "gx":
                    pairs.append((x, target[0])) if y == 0 else None
                elif axes == "gy":
                    pairs.append((y, target[1])) if x == 0 else None
                else:
                    pairs.append((x * down + y, target[0] * down + target[1]))
        flat = part.reshape(-1)
        return lax.ppermute(flat, axes, pairs).reshape(part.shape)

    both = ("gx", "gy")
    top, bottom = (value[..., :width, :], value[..., rows - width :, :])
    left, right = (value[..., :, :width], value[..., :, cols - width :])
    above = shift(bottom, "gy", 0, 1)
    below = shift(top, "gy", 0, -1)
    west = shift(right, "gx", 1, 0)
    east = shift(left, "gx", -1, 0)
    north_west = shift(bottom[..., cols - width :], both, 1, 1)
    north_east = shift(bottom[..., :width], both, -1, 1)
    south_west = shift(top[..., cols - width :], both, 1, -1)
    south_east = shift(top[..., :width], both, -1, -1)
    upper = jnp.concatenate([north_west, above, north_east], axis=-1)
    middle = jnp.concatenate([west, value, east], axis=-1)
    lower = jnp.concatenate([south_west, below, south_east], axis=-1)
    return jnp.concatenate([upper, middle, lower], axis=-2)


def slope_x(padded):
    inner = padded[..., 2:-2, :]
    return (8.0 * (inner[..., 3:-1] - inner[..., 1:-3]) - (inner[..., 4:] - inner[..., :-4])) / 12.0


def slope_y(padded):
    inner = padded[..., :, 2:-2]
    return (
        8.0 * (inner[..., 3:-1, :] - inner[..., 1:-3, :]) - (inner[..., 4:, :] - inner[..., :-4, :])
    ) / 12.0


def center(padded):
    return padded[..., 2:-2, 2:-2]


def tendency(padded, coriolis_parameter):
    wide_h, wide_e, wide_n = (padded[..., 0, :, :], padded[..., 1, :, :], padded[..., 2, :, :])
    east_wind, north_wind = (center(wide_e), center(wide_n))
    depth = mean_depth + wide_h
    change_h = -(slope_x(depth * wide_e) + slope_y(depth * wide_n))
    change_e = (
        -(east_wind * slope_x(wide_e) + north_wind * slope_y(wide_e))
        + coriolis_parameter * north_wind
        - gravity * slope_x(wide_h)
    )
    change_n = (
        -(east_wind * slope_x(wide_n) + north_wind * slope_y(wide_n))
        - coriolis_parameter * east_wind
        - gravity * slope_y(wide_h)
    )
    return jnp.stack([change_h, change_e, change_n], -3)


def body(control, perts):
    tile_rows, tile_column_count = (control.shape[1], control.shape[2])
    grid_rows = tile_rows * lax.axis_size("gy")
    grid_cols = tile_column_count * lax.axis_size("gx")
    first_row = lax.axis_index("gy") * tile_rows

    def coriolis_rows(margin):
        rows = (first_row - margin + jnp.arange(tile_rows + 2 * margin, dtype=jnp.int32)).astype(
            jnp.float32
        )
        return (coriolis_mid * (1.0 + 0.5 * jnp.sin(two_pi * rows / float(grid_rows))))[:, None]

    states = jnp.concatenate([control[None], control[None] + perts], 0)
    margin = 4 * STEPS
    current = with_halo(states, margin)
    for step in range(STEPS):
        first = tendency(current, coriolis_rows(margin - 2))
        middle = current[..., 2:-2, 2:-2] + time_step * first
        second = tendency(middle, coriolis_rows(margin - 4))
        current = current[..., 4:-4, 4:-4] + 0.5 * time_step * (first[..., 2:-2, 2:-2] + second)
        margin = margin - 4
    bred = current[1:] - current[0:1]
    flat = bred.reshape(MEMBERS, -1)
    local_gram = jnp.dot(flat, flat.T, precision=lax.Precision.HIGHEST)
    gram = local_gram
    for axis in ("gx", "gy"):
        count = lax.axis_size(axis)
        if count & (count - 1):
            gram = lax.psum(gram, axis)
            continue
        stride = 1
        while stride < count:
            pairs = [(i, i ^ stride) for i in range(count)]
            gram = gram + lax.ppermute(gram, axis, pairs)
            stride *= 2
    lower = jnp.linalg.cholesky(gram)
    solved = jax.scipy.linalg.solve_triangular(lower, flat, lower=True)
    domain_length = 3 * grid_rows * grid_cols
    basis = (math.sqrt(domain_length) * solved).reshape(perts.shape)
    rfactor = lower.T / math.sqrt(domain_length)
    return (basis, rfactor)


def solution(mesh):
    in_specs = (P(None, "gy", "gx"), P(None, None, "gy", "gx"))
    out_specs = (P(None, None, "gy", "gx"), P())
    return jax.shard_map(body, mesh=mesh, in_specs=in_specs, out_specs=out_specs, check_vma=False)
```

```python
import functools
import math

import jax
import jax.numpy as jnp
from jax import lax
from jax.experimental import pallas as pl
from jax.experimental.pallas import tpu as pltpu
from jax.sharding import PartitionSpec as P

MEMBERS = 16
STEPS = 2


mean_depth = 4.0
gravity = 1.0
coriolis_mid = 0.5
time_step = 0.1
two_pi = 2.0 * math.pi


def ring_halo(value, width, lanes):
    rows, cols = (value.shape[-2], value.shape[-1])
    across, down = (lax.axis_size("gx"), lax.axis_size("gy"))

    def shift(part, axes, dx, dy, flatten=True):
        pairs = []
        for x in range(across):
            for y in range(down):
                target = ((x + dx) % across, (y + dy) % down)
                if axes == "gx":
                    pairs.append((x, target[0])) if y == 0 else None
                elif axes == "gy":
                    pairs.append((y, target[1])) if x == 0 else None
                else:
                    pairs.append((x * down + y, target[0] * down + target[1]))
        if not flatten:
            return lax.ppermute(part, axes, pairs)
        flat = part.reshape(-1)
        return lax.ppermute(flat, axes, pairs).reshape(part.shape)

    both = ("gx", "gy")
    top, bottom = (value[..., :width, :], value[..., rows - width :, :])
    left, right = (value[..., :, :width], value[..., :, cols - width :])
    above = shift(bottom, "gy", 0, 1, flatten=False)
    below = shift(top, "gy", 0, -1, flatten=False)
    west = shift(right, "gx", 1, 0)
    east = shift(left, "gx", -1, 0)
    north_west = shift(bottom[..., cols - width :], both, 1, 1)
    north_east = shift(bottom[..., :width], both, -1, 1)
    south_west = shift(top[..., cols - width :], both, 1, -1)
    south_east = shift(top[..., :width], both, -1, -1)

    def band(centre, east_part, west_part):
        gap = jnp.zeros(centre.shape[:-1] + (lanes - cols - 2 * width,), centre.dtype)
        return jnp.concatenate([centre, east_part, gap, west_part], axis=-1)

    return jnp.concatenate(
        [band(value, east, west), band(below, south_east, south_west), band(above, north_east, north_west)],
        axis=-2,
    )


def forecast_kernel(cor_ref, x_ref, o_ref, *, steps, rows, cols):
    f = cor_ref[...]
    R, C = f.shape
    third = 1.0 / 12.0
    def dx(v):
        g = pltpu.roll(v, C - 1, 1) - pltpu.roll(v, 1, 1)
        w = pltpu.roll(v, C - 2, 1) - pltpu.roll(v, 2, 1)
        return (8.0 * g - w) * third
    def dy(v):
        g = pltpu.roll(v, R - 1, 0) - pltpu.roll(v, 1, 0)
        w = pltpu.roll(v, R - 2, 0) - pltpu.roll(v, 2, 0)
        return (8.0 * g - w) * third
    def tend(h, e, n):
        depth = 4.0 + h
        ch = -(dx(depth * e) + dy(depth * n))
        ce = -(e * dx(e) + n * dy(e)) + f * n - dx(h)
        cn = -(e * dx(n) + n * dy(n)) - f * e - dy(h)
        return ch, ce, cn
    s = (x_ref[0, 0], x_ref[0, 1], x_ref[0, 2])
    for _ in range(steps):
        first = tend(*s)
        mid = tuple(a + 0.1 * b for a, b in zip(s, first))
        second = tend(*mid)
        s = tuple(a + 0.05 * (b + c) for a, b, c in zip(s, first, second))
    for k in range(3):
        o_ref[0, k] = s[k][:rows, :cols]

def forecast(cor, padded, steps, rows, cols):
    S, F, R, C = padded.shape
    return pl.pallas_call(
        functools.partial(forecast_kernel, steps=steps, rows=rows, cols=cols),
        out_shape=jax.ShapeDtypeStruct((S, F, rows, cols), jnp.float32),
        grid=(S,),
        in_specs=[pl.BlockSpec((R, C), lambda i: (0, 0)),
                  pl.BlockSpec((1, F, R, C), lambda i: (i, 0, 0, 0))],
        out_specs=pl.BlockSpec((1, F, rows, cols), lambda i: (i, 0, 0, 0)),
    )(cor, padded)


def body(control, perts):
    tile_rows, tile_column_count = (control.shape[1], control.shape[2])
    grid_rows = tile_rows * lax.axis_size("gy")
    grid_cols = tile_column_count * lax.axis_size("gx")
    first_row = lax.axis_index("gy") * tile_rows
    margin = 4 * STEPS
    lanes = 128 * (-(-(tile_column_count + 2 * margin) // 128))
    ring_rows = tile_rows + 2 * margin
    offsets = jnp.arange(ring_rows, dtype=jnp.int32)
    offsets = jnp.where(offsets < tile_rows + margin, offsets, offsets - ring_rows)
    rows = ((first_row + offsets) % grid_rows).astype(jnp.float32)
    coriolis = coriolis_mid * (1.0 + 0.5 * jnp.sin(two_pi * rows / float(grid_rows)))
    coriolis = jnp.broadcast_to(coriolis[:, None], (ring_rows, lanes))

    states = jnp.concatenate([control[None], control[None] + perts], 0)
    padded = ring_halo(states, margin, lanes)
    current = forecast(coriolis, padded, STEPS, tile_rows, tile_column_count)
    bred = current[1:] - current[0:1]
    flat = bred.reshape(MEMBERS, -1)
    local_gram = jnp.dot(flat, flat.T, precision=lax.Precision.HIGHEST)
    gram = local_gram
    for axis in ("gx", "gy"):
        count = lax.axis_size(axis)
        if count & (count - 1):
            gram = lax.psum(gram, axis)
            continue
        stride = 1
        while stride < count:
            pairs = [(i, i ^ stride) for i in range(count)]
            gram = gram + lax.ppermute(gram, axis, pairs)
            stride *= 2
    lower = jnp.linalg.cholesky(gram)
    solved = jax.scipy.linalg.solve_triangular(lower, flat, lower=True)
    domain_length = 3 * grid_rows * grid_cols
    basis = (math.sqrt(domain_length) * solved).reshape(perts.shape)
    rfactor = lower.T / math.sqrt(domain_length)
    return (basis, rfactor)


def solution(mesh):
    in_specs = (P(None, "gy", "gx"), P(None, None, "gy", "gx"))
    out_specs = (P(None, None, "gy", "gx"), P())
    return jax.shard_map(body, mesh=mesh, in_specs=in_specs, out_specs=out_specs, check_vma=False)
```

```python
import functools
import math

import jax
import jax.numpy as jnp
from jax import lax
from jax.experimental import pallas as pl
from jax.experimental.pallas import tpu as pltpu
from jax.sharding import PartitionSpec as P

MEMBERS = 16
STEPS = 2


mean_depth = 4.0
gravity = 1.0
coriolis_mid = 0.5
time_step = 0.1
two_pi = 2.0 * math.pi


def ring_halo(value, width, lanes):
    rows, cols = (value.shape[-2], value.shape[-1])
    across, down = (lax.axis_size("gx"), lax.axis_size("gy"))

    def shift(part, axes, dx, dy, flatten=True):
        pairs = []
        for x in range(across):
            for y in range(down):
                target = ((x + dx) % across, (y + dy) % down)
                if axes == "gx":
                    pairs.append((x, target[0])) if y == 0 else None
                elif axes == "gy":
                    pairs.append((y, target[1])) if x == 0 else None
                else:
                    pairs.append((x * down + y, target[0] * down + target[1]))
        if not flatten:
            return lax.ppermute(part, axes, pairs)
        flat = part.reshape(-1)
        return lax.ppermute(flat, axes, pairs).reshape(part.shape)

    top, bottom = (value[..., :width, :], value[..., rows - width :, :])
    above = shift(bottom, "gy", 0, 1, flatten=False)
    below = shift(top, "gy", 0, -1, flatten=False)
    tall = jnp.concatenate([value, below, above], axis=-2)
    west = shift(tall[..., cols - width :], "gx", 1, 0)
    east = shift(tall[..., :width], "gx", -1, 0)
    gap = jnp.zeros(tall.shape[:-1] + (lanes - cols - 2 * width,), tall.dtype)
    return jnp.concatenate([tall, east, gap, west], axis=-1)


def forecast_kernel(cor_ref, x_ref, o_ref, *, steps, rows, cols):
    f = cor_ref[...]
    R, C = f.shape
    third = 1.0 / 12.0
    def dx(v):
        g = pltpu.roll(v, C - 1, 1) - pltpu.roll(v, 1, 1)
        w = pltpu.roll(v, C - 2, 1) - pltpu.roll(v, 2, 1)
        return (8.0 * g - w) * third
    def dy(v):
        g = pltpu.roll(v, R - 1, 0) - pltpu.roll(v, 1, 0)
        w = pltpu.roll(v, R - 2, 0) - pltpu.roll(v, 2, 0)
        return (8.0 * g - w) * third
    def tend(h, e, n):
        depth = 4.0 + h
        ch = -(dx(depth * e) + dy(depth * n))
        ce = -(e * dx(e) + n * dy(e)) + f * n - dx(h)
        cn = -(e * dx(n) + n * dy(n)) - f * e - dy(h)
        return ch, ce, cn
    s = (x_ref[0, 0], x_ref[0, 1], x_ref[0, 2])
    for _ in range(steps):
        first = tend(*s)
        mid = tuple(a + 0.1 * b for a, b in zip(s, first))
        second = tend(*mid)
        s = tuple(a + 0.05 * (b + c) for a, b, c in zip(s, first, second))
    for k in range(3):
        o_ref[0, k] = s[k][:rows, :cols]

def forecast(cor, padded, steps, rows, cols):
    S, F, R, C = padded.shape
    return pl.pallas_call(
        functools.partial(forecast_kernel, steps=steps, rows=rows, cols=cols),
        out_shape=jax.ShapeDtypeStruct((S, F, rows, cols), jnp.float32),
        grid=(S,),
        in_specs=[pl.BlockSpec((R, C), lambda i: (0, 0)),
                  pl.BlockSpec((1, F, R, C), lambda i: (i, 0, 0, 0))],
        out_specs=pl.BlockSpec((1, F, rows, cols), lambda i: (i, 0, 0, 0)),
    )(cor, padded)


def body(control, perts):
    tile_rows, tile_column_count = (control.shape[1], control.shape[2])
    grid_rows = tile_rows * lax.axis_size("gy")
    grid_cols = tile_column_count * lax.axis_size("gx")
    first_row = lax.axis_index("gy") * tile_rows
    margin = 4 * STEPS
    lanes = 128 * (-(-(tile_column_count + 2 * margin) // 128))
    ring_rows = tile_rows + 2 * margin
    offsets = jnp.arange(ring_rows, dtype=jnp.int32)
    offsets = jnp.where(offsets < tile_rows + margin, offsets, offsets - ring_rows)
    rows = ((first_row + offsets) % grid_rows).astype(jnp.float32)
    coriolis = coriolis_mid * (1.0 + 0.5 * jnp.sin(two_pi * rows / float(grid_rows)))
    coriolis = jnp.broadcast_to(coriolis[:, None], (ring_rows, lanes))

    states = jnp.concatenate([control[None], control[None] + perts], 0)
    padded = ring_halo(states, margin, lanes)
    current = forecast(coriolis, padded, STEPS, tile_rows, tile_column_count)
    bred = current[1:] - current[0:1]
    flat = bred.reshape(MEMBERS, -1)
    local_gram = jnp.dot(flat, flat.T, precision=lax.Precision.HIGHEST)
    gram = local_gram
    for axis in ("gx", "gy"):
        count = lax.axis_size(axis)
        if count & (count - 1):
            gram = lax.psum(gram, axis)
            continue
        stride = 1
        while stride < count:
            pairs = [(i, i ^ stride) for i in range(count)]
            gram = gram + lax.ppermute(gram, axis, pairs)
            stride *= 2
    lower = jnp.linalg.cholesky(gram)
    solved = jax.scipy.linalg.solve_triangular(lower, flat, lower=True)
    domain_length = 3 * grid_rows * grid_cols
    basis = (math.sqrt(domain_length) * solved).reshape(perts.shape)
    rfactor = lower.T / math.sqrt(domain_length)
    return (basis, rfactor)


def solution(mesh):
    in_specs = (P(None, "gy", "gx"), P(None, None, "gy", "gx"))
    out_specs = (P(None, None, "gy", "gx"), P())
    return jax.shard_map(body, mesh=mesh, in_specs=in_specs, out_specs=out_specs, check_vma=False)
```

```python
import functools
import math

import jax
import jax.numpy as jnp
from jax import lax
from jax.experimental import pallas as pl
from jax.experimental.pallas import tpu as pltpu
from jax.sharding import PartitionSpec as P

MEMBERS = 16
STEPS = 2


mean_depth = 4.0
gravity = 1.0
coriolis_mid = 0.5
time_step = 0.1
two_pi = 2.0 * math.pi


def shift(part, axes, dx, dy, flatten=True):
    across, down = (lax.axis_size("gx"), lax.axis_size("gy"))
    pairs = []
    for x in range(across):
        for y in range(down):
            target = ((x + dx) % across, (y + dy) % down)
            if axes == "gx":
                pairs.append((x, target[0])) if y == 0 else None
            else:
                pairs.append((y, target[1])) if x == 0 else None
    if not flatten:
        return lax.ppermute(part, axes, pairs)
    flat = part.reshape(-1)
    return lax.ppermute(flat, axes, pairs).reshape(part.shape)


def row_halo(value, width):
    rows = value.shape[-2]
    top, bottom = (value[..., :width, :], value[..., rows - width :, :])
    return (shift(bottom, "gy", 0, 1, flatten=False), shift(top, "gy", 0, -1, flatten=False))


def ring_halo(value, above, below, width, lanes):
    cols = value.shape[-1]
    tall = jnp.concatenate([value, below, above], axis=-2)
    west = shift(tall[..., cols - width :], "gx", 1, 0)
    east = shift(tall[..., :width], "gx", -1, 0)
    gap = jnp.zeros(tall.shape[:-1] + (lanes - cols - 2 * width,), tall.dtype)
    return jnp.concatenate([tall, east, gap, west], axis=-1)


def forecast_kernel(cor_ref, x_ref, o_ref, *, steps, rows, cols):
    f = cor_ref[...]
    R, C = f.shape
    third = 1.0 / 12.0
    def dx(v):
        g = pltpu.roll(v, C - 1, 1) - pltpu.roll(v, 1, 1)
        w = pltpu.roll(v, C - 2, 1) - pltpu.roll(v, 2, 1)
        return (8.0 * g - w) * third
    def dy(v):
        g = pltpu.roll(v, R - 1, 0) - pltpu.roll(v, 1, 0)
        w = pltpu.roll(v, R - 2, 0) - pltpu.roll(v, 2, 0)
        return (8.0 * g - w) * third
    def tend(h, e, n):
        depth = 4.0 + h
        ch = -(dx(depth * e) + dy(depth * n))
        ce = -(e * dx(e) + n * dy(e)) + f * n - dx(h)
        cn = -(e * dx(n) + n * dy(n)) - f * e - dy(h)
        return ch, ce, cn
    s = (x_ref[0, 0], x_ref[0, 1], x_ref[0, 2])
    for _ in range(steps):
        first = tend(*s)
        mid = tuple(a + 0.1 * b for a, b in zip(s, first))
        second = tend(*mid)
        s = tuple(a + 0.05 * (b + c) for a, b, c in zip(s, first, second))
    for k in range(3):
        o_ref[0, k] = s[k][:rows, :cols]

def forecast(cor, padded, steps, rows, cols):
    S, F, R, C = padded.shape
    return pl.pallas_call(
        functools.partial(forecast_kernel, steps=steps, rows=rows, cols=cols),
        out_shape=jax.ShapeDtypeStruct((S, F, rows, cols), jnp.float32),
        grid=(S,),
        in_specs=[pl.BlockSpec((R, C), lambda i: (0, 0)),
                  pl.BlockSpec((1, F, R, C), lambda i: (i, 0, 0, 0))],
        out_specs=pl.BlockSpec((1, F, rows, cols), lambda i: (i, 0, 0, 0)),
        cost_estimate=pl.CostEstimate(
            flops=S * F * R * C * 300 * steps, transcendentals=0, bytes_accessed=4 * S * F * (R * C + rows * cols)
        ),
    )(cor, padded)


def body(control, perts):
    tile_rows, tile_column_count = (control.shape[1], control.shape[2])
    grid_rows = tile_rows * lax.axis_size("gy")
    grid_cols = tile_column_count * lax.axis_size("gx")
    first_row = lax.axis_index("gy") * tile_rows
    margin = 4 * STEPS
    lanes = 128 * (-(-(tile_column_count + 2 * margin) // 128))
    ring_rows = tile_rows + 2 * margin
    offsets = jnp.arange(ring_rows, dtype=jnp.int32)
    offsets = jnp.where(offsets < tile_rows + margin, offsets, offsets - ring_rows)
    rows = ((first_row + offsets) % grid_rows).astype(jnp.float32)
    coriolis = coriolis_mid * (1.0 + 0.5 * jnp.sin(two_pi * rows / float(grid_rows)))
    coriolis = jnp.broadcast_to(coriolis[:, None], (ring_rows, lanes))

    states = jnp.concatenate([control[None], control[None] + perts], 0)
    split = (states.shape[0] + 1) // 2
    first_part, second_part = (states[:split], states[split:])
    above, below = row_halo(first_part, margin)
    above, below, second_part = lax.optimization_barrier((above, below, second_part))
    later_above, later_below = row_halo(second_part, margin)
    outputs = []
    for part, up, down_ in ((first_part, above, below), (second_part, later_above, later_below)):
        padded = ring_halo(part, up, down_, margin, lanes)
        outputs.append(forecast(coriolis, padded, STEPS, tile_rows, tile_column_count))
    current = jnp.concatenate(outputs, 0)
    bred = current[1:] - current[0:1]
    flat = bred.reshape(MEMBERS, -1)
    local_gram = jnp.dot(flat, flat.T, precision=lax.Precision.HIGHEST)
    gram = local_gram
    for axis in ("gx", "gy"):
        count = lax.axis_size(axis)
        if count & (count - 1):
            gram = lax.psum(gram, axis)
            continue
        stride = 1
        while stride < count:
            pairs = [(i, i ^ stride) for i in range(count)]
            gram = gram + lax.ppermute(gram, axis, pairs)
            stride *= 2
    lower = jnp.linalg.cholesky(gram)
    solved = jax.scipy.linalg.solve_triangular(lower, flat, lower=True)
    domain_length = 3 * grid_rows * grid_cols
    basis = (math.sqrt(domain_length) * solved).reshape(perts.shape)
    rfactor = lower.T / math.sqrt(domain_length)
    return (basis, rfactor)


def solution(mesh):
    in_specs = (P(None, "gy", "gx"), P(None, None, "gy", "gx"))
    out_specs = (P(None, None, "gy", "gx"), P())
    return jax.shard_map(body, mesh=mesh, in_specs=in_specs, out_specs=out_specs, check_vma=False)
```

```python
import functools
import math

import jax
import jax.numpy as jnp
from jax import lax
from jax.experimental import pallas as pl
from jax.experimental.pallas import tpu as pltpu
from jax.sharding import PartitionSpec as P

MEMBERS = 16
STEPS = 2


mean_depth = 4.0
gravity = 1.0
coriolis_mid = 0.5
time_step = 0.1
two_pi = 2.0 * math.pi


def ring_halo(value, width, lanes):
    rows, cols = (value.shape[-2], value.shape[-1])
    across, down = (lax.axis_size("gx"), lax.axis_size("gy"))

    def shift(part, axes, dx, dy, flatten=True):
        pairs = []
        for x in range(across):
            for y in range(down):
                target = ((x + dx) % across, (y + dy) % down)
                if axes == "gx":
                    pairs.append((x, target[0])) if y == 0 else None
                elif axes == "gy":
                    pairs.append((y, target[1])) if x == 0 else None
                else:
                    pairs.append((x * down + y, target[0] * down + target[1]))
        if not flatten:
            return lax.ppermute(part, axes, pairs)
        flat = part.reshape(-1)
        return lax.ppermute(flat, axes, pairs).reshape(part.shape)

    top, bottom = (value[..., :width, :], value[..., rows - width :, :])
    above = shift(bottom, "gy", 0, 1, flatten=False)
    below = shift(top, "gy", 0, -1, flatten=False)
    tall = jnp.concatenate([value, below, above], axis=-2)
    west = shift(tall[..., cols - width :], "gx", 1, 0)
    east = shift(tall[..., :width], "gx", -1, 0)
    return above, below, west, east


def forecast_kernel(cor_ref, x_ref, up_ref, down_ref, west_ref, east_ref, o_ref, ring, east_pad, west_pad, *, steps):
    rows, cols = (x_ref.shape[-2], x_ref.shape[-1])
    R, C = cor_ref.shape
    width = up_ref.shape[-2]
    spare = C - cols

    @pl.when(pl.program_id(0) == 0)
    def _():
        ring[...] = jnp.zeros_like(ring)
        east_pad[...] = jnp.zeros_like(east_pad)
        west_pad[...] = jnp.zeros_like(west_pad)

    for k in range(3):
        ring[k, :rows, :cols] = x_ref[0, k]
        ring[k, rows : rows + width, :cols] = down_ref[0, k]
        ring[k, rows + width :, :cols] = up_ref[0, k]
        east_pad[:, :width] = east_ref[0, k]
        west_pad[:, :width] = west_ref[0, k]
        ring[k, :, cols:] = east_pad[...] + pltpu.roll(west_pad[...], spare - width, 1)

    f = cor_ref[...]
    third = 1.0 / 12.0

    def dx(v):
        g = pltpu.roll(v, C - 1, 1) - pltpu.roll(v, 1, 1)
        w = pltpu.roll(v, C - 2, 1) - pltpu.roll(v, 2, 1)
        return (8.0 * g - w) * third

    def dy(v):
        g = pltpu.roll(v, R - 1, 0) - pltpu.roll(v, 1, 0)
        w = pltpu.roll(v, R - 2, 0) - pltpu.roll(v, 2, 0)
        return (8.0 * g - w) * third

    def tend(h, e, n):
        depth = 4.0 + h
        ch = -(dx(depth * e) + dy(depth * n))
        ce = -(e * dx(e) + n * dy(e)) + f * n - dx(h)
        cn = -(e * dx(n) + n * dy(n)) - f * e - dy(h)
        return ch, ce, cn

    s = (ring[0], ring[1], ring[2])
    for _ in range(steps):
        first = tend(*s)
        mid = tuple(a + 0.1 * b for a, b in zip(s, first))
        second = tend(*mid)
        s = tuple(a + 0.05 * (b + c) for a, b, c in zip(s, first, second))
    for k in range(3):
        o_ref[0, k] = s[k][:rows, :cols]


def forecast(cor, value, above, below, west, east, steps):
    S, F, rows, cols = value.shape
    R, C = cor.shape
    width = above.shape[-2]
    return pl.pallas_call(
        functools.partial(forecast_kernel, steps=steps),
        out_shape=jax.ShapeDtypeStruct((S, F, rows, cols), jnp.float32),
        grid=(S,),
        in_specs=[
            pl.BlockSpec((R, C), lambda i: (0, 0)),
            pl.BlockSpec((1, F, rows, cols), lambda i: (i, 0, 0, 0)),
            pl.BlockSpec((1, F, width, cols), lambda i: (i, 0, 0, 0)),
            pl.BlockSpec((1, F, width, cols), lambda i: (i, 0, 0, 0)),
            pl.BlockSpec((1, F, R, width), lambda i: (i, 0, 0, 0)),
            pl.BlockSpec((1, F, R, width), lambda i: (i, 0, 0, 0)),
        ],
        out_specs=pl.BlockSpec((1, F, rows, cols), lambda i: (i, 0, 0, 0)),
        scratch_shapes=[
            pltpu.VMEM((F, R, C), jnp.float32),
            pltpu.VMEM((R, C - cols), jnp.float32),
            pltpu.VMEM((R, C - cols), jnp.float32),
        ],
        cost_estimate=pl.CostEstimate(
            flops=S * F * R * C * 300 * steps, transcendentals=0, bytes_accessed=4 * S * F * (R * C + rows * cols)
        ),
    )(cor, value, above, below, west, east)


def body(control, perts):
    tile_rows, tile_column_count = (control.shape[1], control.shape[2])
    grid_rows = tile_rows * lax.axis_size("gy")
    grid_cols = tile_column_count * lax.axis_size("gx")
    first_row = lax.axis_index("gy") * tile_rows
    margin = 4 * STEPS
    lanes = 128 * (-(-(tile_column_count + 2 * margin) // 128))
    ring_rows = tile_rows + 2 * margin
    offsets = jnp.arange(ring_rows, dtype=jnp.int32)
    offsets = jnp.where(offsets < tile_rows + margin, offsets, offsets - ring_rows)
    rows = ((first_row + offsets) % grid_rows).astype(jnp.float32)
    coriolis = coriolis_mid * (1.0 + 0.5 * jnp.sin(two_pi * rows / float(grid_rows)))
    coriolis = jnp.broadcast_to(coriolis[:, None], (ring_rows, lanes))

    states = jnp.concatenate([control[None], control[None] + perts], 0)
    above, below, west, east = ring_halo(states, margin, lanes)
    current = forecast(coriolis, states, above, below, west, east, STEPS)
    bred = current[1:] - current[0:1]
    flat = bred.reshape(MEMBERS, -1)
    local_gram = jnp.dot(flat, flat.T, precision=lax.Precision.HIGHEST)
    gram = local_gram
    for axis in ("gx", "gy"):
        count = lax.axis_size(axis)
        if count & (count - 1):
            gram = lax.psum(gram, axis)
            continue
        stride = 1
        while stride < count:
            pairs = [(i, i ^ stride) for i in range(count)]
            gram = gram + lax.ppermute(gram, axis, pairs)
            stride *= 2
    lower = jnp.linalg.cholesky(gram)
    solved = jax.scipy.linalg.solve_triangular(lower, flat, lower=True)
    domain_length = 3 * grid_rows * grid_cols
    basis = (math.sqrt(domain_length) * solved).reshape(perts.shape)
    rfactor = lower.T / math.sqrt(domain_length)
    return (basis, rfactor)


def solution(mesh):
    in_specs = (P(None, "gy", "gx"), P(None, None, "gy", "gx"))
    out_specs = (P(None, None, "gy", "gx"), P())
    return jax.shard_map(body, mesh=mesh, in_specs=in_specs, out_specs=out_specs, check_vma=False)
```

```python
import functools
import math

import jax
import jax.numpy as jnp
from jax import lax
from jax.experimental import pallas as pl
from jax.experimental.pallas import tpu as pltpu
from jax.sharding import PartitionSpec as P

MEMBERS = 16
STEPS = 2


mean_depth = 4.0
gravity = 1.0
coriolis_mid = 0.5
time_step = 0.1
two_pi = 2.0 * math.pi


def ring_halo(value, width, lanes):
    rows, cols = (value.shape[-2], value.shape[-1])
    across, down = (lax.axis_size("gx"), lax.axis_size("gy"))

    def shift(part, axes, dx, dy, flatten=True):
        pairs = []
        for x in range(across):
            for y in range(down):
                target = ((x + dx) % across, (y + dy) % down)
                if axes == "gx":
                    pairs.append((x, target[0])) if y == 0 else None
                elif axes == "gy":
                    pairs.append((y, target[1])) if x == 0 else None
                else:
                    pairs.append((x * down + y, target[0] * down + target[1]))
        if not flatten:
            return lax.ppermute(part, axes, pairs)
        flat = part.reshape(-1)
        return lax.ppermute(flat, axes, pairs).reshape(part.shape)

    top, bottom = (value[..., :width, :], value[..., rows - width :, :])
    above = shift(bottom, "gy", 0, 1, flatten=False)
    below = shift(top, "gy", 0, -1, flatten=False)
    tall = jnp.concatenate([value, below, above], axis=-2)
    west = shift(tall[..., cols - width :], "gx", 1, 0)
    east = shift(tall[..., :width], "gx", -1, 0)
    return above, below, west, east


def forecast_kernel(cor_ref, x_ref, up_ref, down_ref, west_ref, east_ref, o_ref, ring, east_pad, west_pad, control, *, steps):
    rows, cols = (x_ref.shape[-2], x_ref.shape[-1])
    R, C = cor_ref.shape
    width = up_ref.shape[-2]
    spare = C - cols

    @pl.when(pl.program_id(0) == 0)
    def _():
        ring[...] = jnp.zeros_like(ring)
        east_pad[...] = jnp.zeros_like(east_pad)
        west_pad[...] = jnp.zeros_like(west_pad)

    for k in range(3):
        ring[k, :rows, :cols] = x_ref[0, k]
        ring[k, rows : rows + width, :cols] = down_ref[0, k]
        ring[k, rows + width :, :cols] = up_ref[0, k]
        east_pad[:, :width] = east_ref[0, k]
        west_pad[:, :width] = west_ref[0, k]
        ring[k, :, cols:] = east_pad[...] + pltpu.roll(west_pad[...], spare - width, 1)

    f = cor_ref[...]
    third = 1.0 / 12.0

    def dx(v):
        g = pltpu.roll(v, C - 1, 1) - pltpu.roll(v, 1, 1)
        w = pltpu.roll(v, C - 2, 1) - pltpu.roll(v, 2, 1)
        return (8.0 * g - w) * third

    def dy(v):
        g = pltpu.roll(v, R - 1, 0) - pltpu.roll(v, 1, 0)
        w = pltpu.roll(v, R - 2, 0) - pltpu.roll(v, 2, 0)
        return (8.0 * g - w) * third

    def tend(h, e, n):
        depth = 4.0 + h
        ch = -(dx(depth * e) + dy(depth * n))
        ce = -(e * dx(e) + n * dy(e)) + f * n - dx(h)
        cn = -(e * dx(n) + n * dy(n)) - f * e - dy(h)
        return ch, ce, cn

    s = (ring[0], ring[1], ring[2])
    for _ in range(steps):
        first = tend(*s)
        mid = tuple(a + 0.1 * b for a, b in zip(s, first))
        second = tend(*mid)
        s = tuple(a + 0.05 * (b + c) for a, b, c in zip(s, first, second))
    @pl.when(pl.program_id(0) == 0)
    def _():
        for k in range(3):
            control[k] = s[k][:rows, :cols]

    @pl.when(pl.program_id(0) > 0)
    def _():
        for k in range(3):
            o_ref[0, k] = s[k][:rows, :cols] - control[k]


def forecast(cor, value, above, below, west, east, steps):
    S, F, rows, cols = value.shape
    R, C = cor.shape
    width = above.shape[-2]
    return pl.pallas_call(
        functools.partial(forecast_kernel, steps=steps),
        out_shape=jax.ShapeDtypeStruct((S - 1, F, rows, cols), jnp.float32),
        grid=(S,),
        in_specs=[
            pl.BlockSpec((R, C), lambda i: (0, 0)),
            pl.BlockSpec((1, F, rows, cols), lambda i: (i, 0, 0, 0)),
            pl.BlockSpec((1, F, width, cols), lambda i: (i, 0, 0, 0)),
            pl.BlockSpec((1, F, width, cols), lambda i: (i, 0, 0, 0)),
            pl.BlockSpec((1, F, R, width), lambda i: (i, 0, 0, 0)),
            pl.BlockSpec((1, F, R, width), lambda i: (i, 0, 0, 0)),
        ],
        out_specs=pl.BlockSpec((1, F, rows, cols), lambda i: (jnp.maximum(i - 1, 0), 0, 0, 0)),
        scratch_shapes=[
            pltpu.VMEM((F, R, C), jnp.float32),
            pltpu.VMEM((R, C - cols), jnp.float32),
            pltpu.VMEM((R, C - cols), jnp.float32),
            pltpu.VMEM((F, rows, cols), jnp.float32),
        ],
        cost_estimate=pl.CostEstimate(
            flops=S * F * R * C * 300 * steps, transcendentals=0, bytes_accessed=4 * S * F * (R * C + rows * cols)
        ),
    )(cor, value, above, below, west, east)


def body(control, perts):
    tile_rows, tile_column_count = (control.shape[1], control.shape[2])
    grid_rows = tile_rows * lax.axis_size("gy")
    grid_cols = tile_column_count * lax.axis_size("gx")
    first_row = lax.axis_index("gy") * tile_rows
    margin = 4 * STEPS
    lanes = 128 * (-(-(tile_column_count + 2 * margin) // 128))
    ring_rows = tile_rows + 2 * margin
    offsets = jnp.arange(ring_rows, dtype=jnp.int32)
    offsets = jnp.where(offsets < tile_rows + margin, offsets, offsets - ring_rows)
    rows = ((first_row + offsets) % grid_rows).astype(jnp.float32)
    coriolis = coriolis_mid * (1.0 + 0.5 * jnp.sin(two_pi * rows / float(grid_rows)))
    coriolis = jnp.broadcast_to(coriolis[:, None], (ring_rows, lanes))

    states = jnp.concatenate([control[None], control[None] + perts], 0)
    above, below, west, east = ring_halo(states, margin, lanes)
    bred = forecast(coriolis, states, above, below, west, east, STEPS)
    flat = bred.reshape(MEMBERS, -1)
    local_gram = jnp.dot(flat, flat.T, precision=lax.Precision.HIGHEST)
    gram = local_gram
    for axis in ("gx", "gy"):
        count = lax.axis_size(axis)
        if count & (count - 1):
            gram = lax.psum(gram, axis)
            continue
        stride = 1
        while stride < count:
            pairs = [(i, i ^ stride) for i in range(count)]
            gram = gram + lax.ppermute(gram, axis, pairs)
            stride *= 2
    lower = jnp.linalg.cholesky(gram)
    solved = jax.scipy.linalg.solve_triangular(lower, flat, lower=True)
    domain_length = 3 * grid_rows * grid_cols
    basis = (math.sqrt(domain_length) * solved).reshape(perts.shape)
    rfactor = lower.T / math.sqrt(domain_length)
    return (basis, rfactor)


def solution(mesh):
    in_specs = (P(None, "gy", "gx"), P(None, None, "gy", "gx"))
    out_specs = (P(None, None, "gy", "gx"), P())
    return jax.shard_map(body, mesh=mesh, in_specs=in_specs, out_specs=out_specs, check_vma=False)
```

```python
import functools
import math

import jax
import jax.numpy as jnp
from jax import lax
from jax.experimental import pallas as pl
from jax.experimental.pallas import tpu as pltpu
from jax.sharding import PartitionSpec as P

MEMBERS = 16
STEPS = 2


mean_depth = 4.0
gravity = 1.0
coriolis_mid = 0.5
time_step = 0.1
two_pi = 2.0 * math.pi


def ring_halo(value, width, lanes):
    rows, cols = (value.shape[-2], value.shape[-1])
    across, down = (lax.axis_size("gx"), lax.axis_size("gy"))

    def shift(part, axes, dx, dy, flatten=True):
        pairs = []
        for x in range(across):
            for y in range(down):
                target = ((x + dx) % across, (y + dy) % down)
                if axes == "gx":
                    pairs.append((x, target[0])) if y == 0 else None
                elif axes == "gy":
                    pairs.append((y, target[1])) if x == 0 else None
                else:
                    pairs.append((x * down + y, target[0] * down + target[1]))
        if not flatten:
            return lax.ppermute(part, axes, pairs)
        flat = part.reshape(-1)
        return lax.ppermute(flat, axes, pairs).reshape(part.shape)

    top, bottom = (value[..., :width, :], value[..., rows - width :, :])
    above = shift(bottom, "gy", 0, 1, flatten=False)
    below = shift(top, "gy", 0, -1, flatten=False)
    tall = jnp.concatenate([value, below, above], axis=-2)
    west = shift(tall[..., cols - width :], "gx", 1, 0)
    east = shift(tall[..., :width], "gx", -1, 0)
    return above, below, west, east


def forecast_kernel(cor_ref, x_ref, up_ref, down_ref, west_ref, east_ref, o_ref, ring, east_pad, west_pad, control, *, steps):
    rows, cols = (x_ref.shape[-2], x_ref.shape[-1])
    R, C = cor_ref.shape
    width = up_ref.shape[-2]
    spare = C - cols

    @pl.when(pl.program_id(0) == 0)
    def _():
        ring[...] = jnp.zeros_like(ring)
        east_pad[...] = jnp.zeros_like(east_pad)
        west_pad[...] = jnp.zeros_like(west_pad)

    for k in range(3):
        ring[k, :rows, :cols] = x_ref[0, k]
        ring[k, rows : rows + width, :cols] = down_ref[0, k]
        ring[k, rows + width :, :cols] = up_ref[0, k]
        east_pad[:, :width] = east_ref[0, k]
        west_pad[:, :width] = west_ref[0, k]
        ring[k, :, cols:] = east_pad[...] + pltpu.roll(west_pad[...], spare - width, 1)

    f = cor_ref[...]
    third = 1.0 / 12.0

    def dx(v):
        g = pltpu.roll(v, C - 1, 1) - pltpu.roll(v, 1, 1)
        w = pltpu.roll(v, C - 2, 1) - pltpu.roll(v, 2, 1)
        return (8.0 * g - w) * third

    def dy(v):
        g = pltpu.roll(v, R - 1, 0) - pltpu.roll(v, 1, 0)
        w = pltpu.roll(v, R - 2, 0) - pltpu.roll(v, 2, 0)
        return (8.0 * g - w) * third

    def tend(h, e, n):
        depth = 4.0 + h
        ch = -(dx(depth * e) + dy(depth * n))
        ce = -(e * dx(e) + n * dy(e)) + f * n - dx(h)
        cn = -(e * dx(n) + n * dy(n)) - f * e - dy(h)
        return ch, ce, cn

    s = (ring[0], ring[1], ring[2])
    for _ in range(steps):
        first = tend(*s)
        mid = tuple(a + 0.1 * b for a, b in zip(s, first))
        second = tend(*mid)
        s = tuple(a + 0.05 * (b + c) for a, b, c in zip(s, first, second))
    @pl.when(pl.program_id(0) == 0)
    def _():
        for k in range(3):
            control[k] = s[k][:rows, :cols]

    @pl.when(pl.program_id(0) > 0)
    def _():
        for k in range(3):
            o_ref[0, k] = s[k][:rows, :cols] - control[k]


def forecast(cor, value, above, below, west, east, steps):
    S, F, rows, cols = value.shape
    R, C = cor.shape
    width = above.shape[-2]
    return pl.pallas_call(
        functools.partial(forecast_kernel, steps=steps),
        out_shape=jax.ShapeDtypeStruct((S - 1, F, rows, cols), jnp.float32),
        grid=(S,),
        in_specs=[
            pl.BlockSpec((R, C), lambda i: (0, 0)),
            pl.BlockSpec((1, F, rows, cols), lambda i: (i, 0, 0, 0)),
            pl.BlockSpec((1, F, width, cols), lambda i: (i, 0, 0, 0)),
            pl.BlockSpec((1, F, width, cols), lambda i: (i, 0, 0, 0)),
            pl.BlockSpec((1, F, R, width), lambda i: (i, 0, 0, 0)),
            pl.BlockSpec((1, F, R, width), lambda i: (i, 0, 0, 0)),
        ],
        out_specs=pl.BlockSpec((1, F, rows, cols), lambda i: (jnp.maximum(i - 1, 0), 0, 0, 0)),
        scratch_shapes=[
            pltpu.VMEM((F, R, C), jnp.float32),
            pltpu.VMEM((R, C - cols), jnp.float32),
            pltpu.VMEM((R, C - cols), jnp.float32),
            pltpu.VMEM((F, rows, cols), jnp.float32),
        ],
        cost_estimate=pl.CostEstimate(
            flops=S * F * R * C * 300 * steps, transcendentals=0, bytes_accessed=4 * S * F * (R * C + rows * cols)
        ),
    )(cor, value, above, below, west, east)


def body(control, perts):
    tile_rows, tile_column_count = (control.shape[1], control.shape[2])
    grid_rows = tile_rows * lax.axis_size("gy")
    grid_cols = tile_column_count * lax.axis_size("gx")
    first_row = lax.axis_index("gy") * tile_rows
    margin = 4 * STEPS
    lanes = 128 * (-(-(tile_column_count + 2 * margin) // 128))
    ring_rows = tile_rows + 2 * margin
    offsets = jnp.arange(ring_rows, dtype=jnp.int32)
    offsets = jnp.where(offsets < tile_rows + margin, offsets, offsets - ring_rows)
    rows = ((first_row + offsets) % grid_rows).astype(jnp.float32)
    coriolis = coriolis_mid * (1.0 + 0.5 * jnp.sin(two_pi * rows / float(grid_rows)))
    coriolis = jnp.broadcast_to(coriolis[:, None], (ring_rows, lanes))

    states = jnp.concatenate([control[None], control[None] + perts], 0)
    above, below, west, east = ring_halo(states, margin, lanes)
    bred = forecast(coriolis, states, above, below, west, east, STEPS)
    local_gram = jnp.einsum("ifrc,jfrc->ij", bred, bred, precision=lax.Precision.HIGHEST)
    gram = local_gram
    for axis in ("gx", "gy"):
        count = lax.axis_size(axis)
        if count & (count - 1):
            gram = lax.psum(gram, axis)
            continue
        stride = 1
        while stride < count:
            pairs = [(i, i ^ stride) for i in range(count)]
            gram = gram + lax.ppermute(gram, axis, pairs)
            stride *= 2
    lower = jnp.linalg.cholesky(gram)
    members = bred.shape[0]
    inverse = jax.scipy.linalg.solve_triangular(lower, jnp.eye(members, dtype=lower.dtype), lower=True)
    domain_length = 3 * grid_rows * grid_cols
    solved = jnp.einsum("ij,jfrc->ifrc", inverse, bred, precision=lax.Precision.HIGHEST)
    basis = math.sqrt(domain_length) * solved
    rfactor = lower.T / math.sqrt(domain_length)
    return (basis, rfactor)


def solution(mesh):
    in_specs = (P(None, "gy", "gx"), P(None, None, "gy", "gx"))
    out_specs = (P(None, None, "gy", "gx"), P())
    return jax.shard_map(body, mesh=mesh, in_specs=in_specs, out_specs=out_specs, check_vma=False)
```

```python
import functools
import math

import jax
import jax.numpy as jnp
from jax import lax
from jax.experimental import pallas as pl
from jax.experimental.pallas import tpu as pltpu
from jax.sharding import PartitionSpec as P

MEMBERS = 16
STEPS = 2


mean_depth = 4.0
gravity = 1.0
coriolis_mid = 0.5
time_step = 0.1
two_pi = 2.0 * math.pi


def row_halo(value, width):
    rows = value.shape[-2]
    top, bottom = (value[..., :width, :], value[..., rows - width :, :])
    return (shift(bottom, "gy", 0, 1, flatten=False), shift(top, "gy", 0, -1, flatten=False))


def column_halo(value, above, below, width):
    cols = value.shape[-1]
    tall = jnp.concatenate([value, below, above], axis=-2)
    return (shift(tall[..., cols - width :], "gx", 1, 0), shift(tall[..., :width], "gx", -1, 0))


def shift(part, axes, dx, dy, flatten=True):
    across, down = (lax.axis_size("gx"), lax.axis_size("gy"))
    pairs = []
    for x in range(across):
        for y in range(down):
            target = ((x + dx) % across, (y + dy) % down)
            if axes == "gx":
                pairs.append((x, target[0])) if y == 0 else None
            else:
                pairs.append((y, target[1])) if x == 0 else None
    if not flatten:
        return lax.ppermute(part, axes, pairs)
    flat = part.reshape(-1)
    return lax.ppermute(flat, axes, pairs).reshape(part.shape)


def forecast_kernel(cor_ref, x_ref, up_ref, down_ref, west_ref, east_ref, o_ref, ring, east_pad, west_pad, *, steps):
    rows, cols = (x_ref.shape[-2], x_ref.shape[-1])
    R, C = cor_ref.shape
    width = up_ref.shape[-2]
    spare = C - cols

    @pl.when(pl.program_id(0) == 0)
    def _():
        ring[...] = jnp.zeros_like(ring)
        east_pad[...] = jnp.zeros_like(east_pad)
        west_pad[...] = jnp.zeros_like(west_pad)

    for k in range(3):
        ring[k, :rows, :cols] = x_ref[0, k]
        ring[k, rows : rows + width, :cols] = down_ref[0, k]
        ring[k, rows + width :, :cols] = up_ref[0, k]
        east_pad[:, :width] = east_ref[0, k]
        west_pad[:, :width] = west_ref[0, k]
        ring[k, :, cols:] = east_pad[...] + pltpu.roll(west_pad[...], spare - width, 1)

    f = cor_ref[...]
    third = 1.0 / 12.0

    def dx(v):
        g = pltpu.roll(v, C - 1, 1) - pltpu.roll(v, 1, 1)
        w = pltpu.roll(v, C - 2, 1) - pltpu.roll(v, 2, 1)
        return (8.0 * g - w) * third

    def dy(v):
        g = pltpu.roll(v, R - 1, 0) - pltpu.roll(v, 1, 0)
        w = pltpu.roll(v, R - 2, 0) - pltpu.roll(v, 2, 0)
        return (8.0 * g - w) * third

    def tend(h, e, n):
        depth = 4.0 + h
        ch = -(dx(depth * e) + dy(depth * n))
        ce = -(e * dx(e) + n * dy(e)) + f * n - dx(h)
        cn = -(e * dx(n) + n * dy(n)) - f * e - dy(h)
        return ch, ce, cn

    s = (ring[0], ring[1], ring[2])
    for _ in range(steps):
        first = tend(*s)
        mid = tuple(a + 0.1 * b for a, b in zip(s, first))
        second = tend(*mid)
        s = tuple(a + 0.05 * (b + c) for a, b, c in zip(s, first, second))
    for k in range(3):
        o_ref[0, k] = s[k][:rows, :cols]


def forecast(cor, value, above, below, west, east, steps):
    S, F, rows, cols = value.shape
    R, C = cor.shape
    width = above.shape[-2]
    return pl.pallas_call(
        functools.partial(forecast_kernel, steps=steps),
        out_shape=jax.ShapeDtypeStruct((S, F, rows, cols), jnp.float32),
        grid=(S,),
        in_specs=[
            pl.BlockSpec((R, C), lambda i: (0, 0)),
            pl.BlockSpec((1, F, rows, cols), lambda i: (i, 0, 0, 0)),
            pl.BlockSpec((1, F, width, cols), lambda i: (i, 0, 0, 0)),
            pl.BlockSpec((1, F, width, cols), lambda i: (i, 0, 0, 0)),
            pl.BlockSpec((1, F, R, width), lambda i: (i, 0, 0, 0)),
            pl.BlockSpec((1, F, R, width), lambda i: (i, 0, 0, 0)),
        ],
        out_specs=pl.BlockSpec((1, F, rows, cols), lambda i: (i, 0, 0, 0)),
        scratch_shapes=[
            pltpu.VMEM((F, R, C), jnp.float32),
            pltpu.VMEM((R, C - cols), jnp.float32),
            pltpu.VMEM((R, C - cols), jnp.float32),
        ],
        cost_estimate=pl.CostEstimate(
            flops=S * F * R * C * 300 * steps, transcendentals=0, bytes_accessed=4 * S * F * (R * C + rows * cols)
        ),
    )(cor, value, above, below, west, east)


def body(control, perts):
    tile_rows, tile_column_count = (control.shape[1], control.shape[2])
    grid_rows = tile_rows * lax.axis_size("gy")
    grid_cols = tile_column_count * lax.axis_size("gx")
    first_row = lax.axis_index("gy") * tile_rows
    margin = 4 * STEPS
    lanes = 128 * (-(-(tile_column_count + 2 * margin) // 128))
    ring_rows = tile_rows + 2 * margin
    offsets = jnp.arange(ring_rows, dtype=jnp.int32)
    offsets = jnp.where(offsets < tile_rows + margin, offsets, offsets - ring_rows)
    rows = ((first_row + offsets) % grid_rows).astype(jnp.float32)
    coriolis = coriolis_mid * (1.0 + 0.5 * jnp.sin(two_pi * rows / float(grid_rows)))
    coriolis = jnp.broadcast_to(coriolis[:, None], (ring_rows, lanes))

    states = jnp.concatenate([control[None], control[None] + perts], 0)
    split = (states.shape[0] + 1) // 2
    first_part, second_part = (states[:split], states[split:])
    above, below = row_halo(first_part, margin)
    above, below, second_part = lax.optimization_barrier((above, below, second_part))
    later_above, later_below = row_halo(second_part, margin)
    outputs = []
    for part, up, down_ in ((first_part, above, below), (second_part, later_above, later_below)):
        west, east = column_halo(part, up, down_, margin)
        outputs.append(forecast(coriolis, part, up, down_, west, east, STEPS))
    current = jnp.concatenate(outputs, 0)
    bred = current[1:] - current[0:1]
    flat = bred.reshape(MEMBERS, -1)
    local_gram = jnp.dot(flat, flat.T, precision=lax.Precision.HIGHEST)
    gram = local_gram
    for axis in ("gx", "gy"):
        count = lax.axis_size(axis)
        if count & (count - 1):
            gram = lax.psum(gram, axis)
            continue
        stride = 1
        while stride < count:
            pairs = [(i, i ^ stride) for i in range(count)]
            gram = gram + lax.ppermute(gram, axis, pairs)
            stride *= 2
    lower = jnp.linalg.cholesky(gram)
    solved = jax.scipy.linalg.solve_triangular(lower, flat, lower=True)
    domain_length = 3 * grid_rows * grid_cols
    basis = (math.sqrt(domain_length) * solved).reshape(perts.shape)
    rfactor = lower.T / math.sqrt(domain_length)
    return (basis, rfactor)


def solution(mesh):
    in_specs = (P(None, "gy", "gx"), P(None, None, "gy", "gx"))
    out_specs = (P(None, None, "gy", "gx"), P())
    return jax.shard_map(body, mesh=mesh, in_specs=in_specs, out_specs=out_specs, check_vma=False)
```

```python
import functools
import math

import jax
import jax.numpy as jnp
from jax import lax
from jax.experimental import pallas as pl
from jax.experimental.pallas import tpu as pltpu
from jax.sharding import PartitionSpec as P

MEMBERS = 16
STEPS = 2


mean_depth = 4.0
gravity = 1.0
coriolis_mid = 0.5
time_step = 0.1
two_pi = 2.0 * math.pi


def ring_halo(value, width, lanes):
    rows, cols = (value.shape[-2], value.shape[-1])
    across, down = (lax.axis_size("gx"), lax.axis_size("gy"))

    def shift(part, axes, dx, dy, flatten=True):
        pairs = []
        for x in range(across):
            for y in range(down):
                target = ((x + dx) % across, (y + dy) % down)
                if axes == "gx":
                    pairs.append((x, target[0])) if y == 0 else None
                elif axes == "gy":
                    pairs.append((y, target[1])) if x == 0 else None
                else:
                    pairs.append((x * down + y, target[0] * down + target[1]))
        if not flatten:
            return lax.ppermute(part, axes, pairs)
        flat = part.reshape(-1)
        return lax.ppermute(flat, axes, pairs).reshape(part.shape)

    top, bottom = (value[..., :width, :], value[..., rows - width :, :])
    above = shift(bottom, "gy", 0, 1, flatten=False)
    below = shift(top, "gy", 0, -1, flatten=False)
    tall = jnp.concatenate([value, below, above], axis=-2)
    west = shift(tall[..., cols - width :], "gx", 1, 0)
    east = shift(tall[..., :width], "gx", -1, 0)
    return above, below, west, east


def forecast_kernel(cor_ref, x_ref, up_ref, down_ref, west_ref, east_ref, o_ref, ring, east_pad, west_pad, *, steps):
    rows, cols = (x_ref.shape[-2], x_ref.shape[-1])
    R, C = ring.shape[-2:]
    width = up_ref.shape[-2]
    spare = C - cols

    @pl.when(pl.program_id(0) == 0)
    def _():
        ring[...] = jnp.zeros_like(ring)
        east_pad[...] = jnp.zeros_like(east_pad)
        west_pad[...] = jnp.zeros_like(west_pad)

    for k in range(3):
        ring[k, :rows, :cols] = x_ref[0, k]
        ring[k, rows : rows + width, :cols] = down_ref[0, k]
        ring[k, rows + width :, :cols] = up_ref[0, k]
        east_pad[:, :width] = east_ref[0, k]
        west_pad[:, :width] = west_ref[0, k]
        ring[k, :, cols:] = east_pad[...] + pltpu.roll(west_pad[...], spare - width, 1)

    f = jnp.broadcast_to(cor_ref[...], (R, C))
    scale = -1.0 / 12.0

    def dx(v):
        g = pltpu.roll(v, C - 1, 1) - pltpu.roll(v, 1, 1)
        w = pltpu.roll(v, C - 2, 1) - pltpu.roll(v, 2, 1)
        return 8.0 * g - w

    def dy(v):
        g = pltpu.roll(v, R - 1, 0) - pltpu.roll(v, 1, 0)
        w = pltpu.roll(v, R - 2, 0) - pltpu.roll(v, 2, 0)
        return 8.0 * g - w

    def tend(h, e, n):
        depth = 4.0 + h
        ch = scale * (dx(depth * e) + dy(depth * n))
        ce = scale * (e * dx(e) + n * dy(e) + dx(h)) + f * n
        cn = scale * (e * dx(n) + n * dy(n) + dy(h)) - f * e
        return ch, ce, cn

    s = (ring[0], ring[1], ring[2])
    for _ in range(steps):
        first = tend(*s)
        mid = tuple(a + 0.1 * b for a, b in zip(s, first))
        second = tend(*mid)
        s = tuple(a + 0.05 * (b + c) for a, b, c in zip(s, first, second))
    for k in range(3):
        o_ref[0, k] = s[k][:rows, :cols]


def forecast(cor, value, above, below, west, east, steps, lanes):
    S, F, rows, cols = value.shape
    width = above.shape[-2]
    R, C = (cor.shape[0], lanes)
    return pl.pallas_call(
        functools.partial(forecast_kernel, steps=steps),
        out_shape=jax.ShapeDtypeStruct((S, F, rows, cols), jnp.float32),
        grid=(S,),
        in_specs=[
            pl.BlockSpec((R, 1), lambda i: (0, 0)),
            pl.BlockSpec((1, F, rows, cols), lambda i: (i, 0, 0, 0)),
            pl.BlockSpec((1, F, width, cols), lambda i: (i, 0, 0, 0)),
            pl.BlockSpec((1, F, width, cols), lambda i: (i, 0, 0, 0)),
            pl.BlockSpec((1, F, R, width), lambda i: (i, 0, 0, 0)),
            pl.BlockSpec((1, F, R, width), lambda i: (i, 0, 0, 0)),
        ],
        out_specs=pl.BlockSpec((1, F, rows, cols), lambda i: (i, 0, 0, 0)),
        scratch_shapes=[
            pltpu.VMEM((F, R, C), jnp.float32),
            pltpu.VMEM((R, C - cols), jnp.float32),
            pltpu.VMEM((R, C - cols), jnp.float32),
        ],
        cost_estimate=pl.CostEstimate(
            flops=S * F * R * C * 300 * steps, transcendentals=0, bytes_accessed=4 * S * F * (R * C + rows * cols)
        ),
    )(cor, value, above, below, west, east)


def body(control, perts):
    tile_rows, tile_column_count = (control.shape[1], control.shape[2])
    grid_rows = tile_rows * lax.axis_size("gy")
    grid_cols = tile_column_count * lax.axis_size("gx")
    first_row = lax.axis_index("gy") * tile_rows
    margin = 4 * STEPS
    lanes = 128 * (-(-(tile_column_count + 2 * margin) // 128))
    ring_rows = tile_rows + 2 * margin
    offsets = jnp.arange(ring_rows, dtype=jnp.int32)
    offsets = jnp.where(offsets < tile_rows + margin, offsets, offsets - ring_rows)
    rows = ((first_row + offsets) % grid_rows).astype(jnp.float32)
    coriolis = coriolis_mid * (1.0 + 0.5 * jnp.sin(two_pi * rows / float(grid_rows)))
    coriolis = coriolis[:, None]

    states = jnp.concatenate([control[None], control[None] + perts], 0)
    above, below, west, east = ring_halo(states, margin, lanes)
    current = forecast(coriolis, states, above, below, west, east, STEPS, lanes)
    bred = current[1:] - current[0:1]
    flat = bred.reshape(MEMBERS, -1)
    local_gram = jnp.dot(flat, flat.T, precision=lax.Precision.HIGHEST)
    gram = local_gram
    for axis in ("gx", "gy"):
        count = lax.axis_size(axis)
        if count & (count - 1):
            gram = lax.psum(gram, axis)
            continue
        stride = 1
        while stride < count:
            pairs = [(i, i ^ stride) for i in range(count)]
            gram = gram + lax.ppermute(gram, axis, pairs)
            stride *= 2
    lower = jnp.linalg.cholesky(gram)
    solved = jax.scipy.linalg.solve_triangular(lower, flat, lower=True)
    domain_length = 3 * grid_rows * grid_cols
    basis = (math.sqrt(domain_length) * solved).reshape(perts.shape)
    rfactor = lower.T / math.sqrt(domain_length)
    return (basis, rfactor)


def solution(mesh):
    in_specs = (P(None, "gy", "gx"), P(None, None, "gy", "gx"))
    out_specs = (P(None, None, "gy", "gx"), P())
    return jax.shard_map(body, mesh=mesh, in_specs=in_specs, out_specs=out_specs, check_vma=False)
```

```python
import functools
import math

import jax
import jax.numpy as jnp
from jax import lax
from jax.experimental import pallas as pl
from jax.experimental.pallas import tpu as pltpu
from jax.sharding import PartitionSpec as P

MEMBERS = 16
STEPS = 2


mean_depth = 4.0
gravity = 1.0
coriolis_mid = 0.5
time_step = 0.1
two_pi = 2.0 * math.pi


def ring_halo(value, width, lanes):
    rows, cols = (value.shape[-2], value.shape[-1])
    across, down = (lax.axis_size("gx"), lax.axis_size("gy"))

    def shift(part, axes, dx, dy, flatten=True):
        pairs = []
        for x in range(across):
            for y in range(down):
                target = ((x + dx) % across, (y + dy) % down)
                if axes == "gx":
                    pairs.append((x, target[0])) if y == 0 else None
                elif axes == "gy":
                    pairs.append((y, target[1])) if x == 0 else None
                else:
                    pairs.append((x * down + y, target[0] * down + target[1]))
        if not flatten:
            return lax.ppermute(part, axes, pairs)
        flat = part.reshape(-1)
        return lax.ppermute(flat, axes, pairs).reshape(part.shape)

    top, bottom = (value[..., :width, :], value[..., rows - width :, :])
    above = shift(bottom, "gy", 0, 1, flatten=False)
    below = shift(top, "gy", 0, -1, flatten=False)
    tall = jnp.concatenate([value, below, above], axis=-2)
    west = shift(jnp.swapaxes(tall[..., cols - width :], -1, -2), "gx", 1, 0, flatten=False)
    east = shift(jnp.swapaxes(tall[..., :width], -1, -2), "gx", -1, 0, flatten=False)
    return above, below, west, east


def forecast_kernel(cor_ref, x_ref, up_ref, down_ref, west_ref, east_ref, o_ref, ring, east_pad, west_pad, *, steps):
    rows, cols = (x_ref.shape[-2], x_ref.shape[-1])
    R, C = cor_ref.shape
    width = up_ref.shape[-2]
    spare = C - cols

    @pl.when(pl.program_id(0) == 0)
    def _():
        ring[...] = jnp.zeros_like(ring)
        east_pad[...] = jnp.zeros_like(east_pad)
        west_pad[...] = jnp.zeros_like(west_pad)

    for k in range(3):
        ring[k, :rows, :cols] = x_ref[0, k]
        ring[k, rows : rows + width, :cols] = down_ref[0, k]
        ring[k, rows + width :, :cols] = up_ref[0, k]
        east_pad[:, :width] = jnp.transpose(east_ref[0, k])
        west_pad[:, :width] = jnp.transpose(west_ref[0, k])
        ring[k, :, cols:] = east_pad[...] + pltpu.roll(west_pad[...], spare - width, 1)

    f = cor_ref[...]
    third = 1.0 / 12.0

    def dx(v):
        g = pltpu.roll(v, C - 1, 1) - pltpu.roll(v, 1, 1)
        w = pltpu.roll(v, C - 2, 1) - pltpu.roll(v, 2, 1)
        return (8.0 * g - w) * third

    def dy(v):
        g = pltpu.roll(v, R - 1, 0) - pltpu.roll(v, 1, 0)
        w = pltpu.roll(v, R - 2, 0) - pltpu.roll(v, 2, 0)
        return (8.0 * g - w) * third

    def tend(h, e, n):
        depth = 4.0 + h
        ch = -(dx(depth * e) + dy(depth * n))
        ce = -(e * dx(e) + n * dy(e)) + f * n - dx(h)
        cn = -(e * dx(n) + n * dy(n)) - f * e - dy(h)
        return ch, ce, cn

    s = (ring[0], ring[1], ring[2])
    for _ in range(steps):
        first = tend(*s)
        mid = tuple(a + 0.1 * b for a, b in zip(s, first))
        second = tend(*mid)
        s = tuple(a + 0.05 * (b + c) for a, b, c in zip(s, first, second))
    for k in range(3):
        o_ref[0, k] = s[k][:rows, :cols]


def forecast(cor, value, above, below, west, east, steps):
    S, F, rows, cols = value.shape
    R, C = cor.shape
    width = above.shape[-2]
    return pl.pallas_call(
        functools.partial(forecast_kernel, steps=steps),
        out_shape=jax.ShapeDtypeStruct((S, F, rows, cols), jnp.float32),
        grid=(S,),
        in_specs=[
            pl.BlockSpec((R, C), lambda i: (0, 0)),
            pl.BlockSpec((1, F, rows, cols), lambda i: (i, 0, 0, 0)),
            pl.BlockSpec((1, F, width, cols), lambda i: (i, 0, 0, 0)),
            pl.BlockSpec((1, F, width, cols), lambda i: (i, 0, 0, 0)),
            pl.BlockSpec((1, F, width, R), lambda i: (i, 0, 0, 0)),
            pl.BlockSpec((1, F, width, R), lambda i: (i, 0, 0, 0)),
        ],
        out_specs=pl.BlockSpec((1, F, rows, cols), lambda i: (i, 0, 0, 0)),
        scratch_shapes=[
            pltpu.VMEM((F, R, C), jnp.float32),
            pltpu.VMEM((R, C - cols), jnp.float32),
            pltpu.VMEM((R, C - cols), jnp.float32),
        ],
        cost_estimate=pl.CostEstimate(
            flops=S * F * R * C * 300 * steps, transcendentals=0, bytes_accessed=4 * S * F * (R * C + rows * cols)
        ),
    )(cor, value, above, below, west, east)


def body(control, perts):
    tile_rows, tile_column_count = (control.shape[1], control.shape[2])
    grid_rows = tile_rows * lax.axis_size("gy")
    grid_cols = tile_column_count * lax.axis_size("gx")
    first_row = lax.axis_index("gy") * tile_rows
    margin = 4 * STEPS
    lanes = 128 * (-(-(tile_column_count + 2 * margin) // 128))
    ring_rows = tile_rows + 2 * margin
    offsets = jnp.arange(ring_rows, dtype=jnp.int32)
    offsets = jnp.where(offsets < tile_rows + margin, offsets, offsets - ring_rows)
    rows = ((first_row + offsets) % grid_rows).astype(jnp.float32)
    coriolis = coriolis_mid * (1.0 + 0.5 * jnp.sin(two_pi * rows / float(grid_rows)))
    coriolis = jnp.broadcast_to(coriolis[:, None], (ring_rows, lanes))

    states = jnp.concatenate([control[None], control[None] + perts], 0)
    above, below, west, east = ring_halo(states, margin, lanes)
    current = forecast(coriolis, states, above, below, west, east, STEPS)
    bred = current[1:] - current[0:1]
    flat = bred.reshape(MEMBERS, -1)
    local_gram = jnp.dot(flat, flat.T, precision=lax.Precision.HIGHEST)
    gram = local_gram
    for axis in ("gx", "gy"):
        count = lax.axis_size(axis)
        if count & (count - 1):
            gram = lax.psum(gram, axis)
            continue
        stride = 1
        while stride < count:
            pairs = [(i, i ^ stride) for i in range(count)]
            gram = gram + lax.ppermute(gram, axis, pairs)
            stride *= 2
    lower = jnp.linalg.cholesky(gram)
    solved = jax.scipy.linalg.solve_triangular(lower, flat, lower=True)
    domain_length = 3 * grid_rows * grid_cols
    basis = (math.sqrt(domain_length) * solved).reshape(perts.shape)
    rfactor = lower.T / math.sqrt(domain_length)
    return (basis, rfactor)


def solution(mesh):
    in_specs = (P(None, "gy", "gx"), P(None, None, "gy", "gx"))
    out_specs = (P(None, None, "gy", "gx"), P())
    return jax.shard_map(body, mesh=mesh, in_specs=in_specs, out_specs=out_specs, check_vma=False)
```

```python
import functools
import math

import jax
import jax.numpy as jnp
from jax import lax
from jax.experimental import pallas as pl
from jax.experimental.pallas import tpu as pltpu
from jax.sharding import PartitionSpec as P

MEMBERS = 16
STEPS = 2


mean_depth = 4.0
gravity = 1.0
coriolis_mid = 0.5
time_step = 0.1
two_pi = 2.0 * math.pi


def ring_halo(value, width, lanes):
    rows, cols = (value.shape[-2], value.shape[-1])
    across, down = (lax.axis_size("gx"), lax.axis_size("gy"))

    def shift(part, axes, dx, dy, flatten=True):
        pairs = []
        for x in range(across):
            for y in range(down):
                target = ((x + dx) % across, (y + dy) % down)
                if axes == "gx":
                    pairs.append((x, target[0])) if y == 0 else None
                elif axes == "gy":
                    pairs.append((y, target[1])) if x == 0 else None
                else:
                    pairs.append((x * down + y, target[0] * down + target[1]))
        if not flatten:
            return lax.ppermute(part, axes, pairs)
        flat = part.reshape(-1)
        return lax.ppermute(flat, axes, pairs).reshape(part.shape)

    top, bottom = (value[..., :width, :], value[..., rows - width :, :])
    above = shift(bottom, "gy", 0, 1, flatten=False)
    below = shift(top, "gy", 0, -1, flatten=False)
    tall = jnp.concatenate([value, below, above], axis=-2)
    west = shift(tall[..., cols - width :], "gx", 1, 0)
    east = shift(tall[..., :width], "gx", -1, 0)
    return above, below, west, east


def forecast_kernel(cor_ref, x_ref, up_ref, down_ref, west_ref, east_ref, o_ref, ring, east_pad, west_pad, *, steps):
    rows, cols = (x_ref.shape[-2], x_ref.shape[-1])
    R, C = cor_ref.shape
    width = up_ref.shape[-2]
    spare = C - cols

    @pl.when(pl.program_id(0) == 0)
    def _():
        ring[...] = jnp.zeros_like(ring)
        east_pad[...] = jnp.zeros_like(east_pad)
        west_pad[...] = jnp.zeros_like(west_pad)

    for k in range(3):
        ring[k, :rows, :cols] = x_ref[0, k]
        ring[k, rows : rows + width, :cols] = down_ref[0, k]
        ring[k, rows + width :, :cols] = up_ref[0, k]
        east_pad[:, :width] = east_ref[0, k]
        west_pad[:, :width] = west_ref[0, k]
        ring[k, :, cols:] = east_pad[...] + pltpu.roll(west_pad[...], spare - width, 1)

    f = cor_ref[...]
    third = 1.0 / 12.0

    def dx(v):
        n_ = v.shape[1]
        g = pltpu.roll(v, n_ - 1, 1) - pltpu.roll(v, 1, 1)
        w = pltpu.roll(v, n_ - 2, 1) - pltpu.roll(v, 2, 1)
        return (8.0 * g - w) * third

    def dy(v):
        n_ = v.shape[0]
        g = pltpu.roll(v, n_ - 1, 0) - pltpu.roll(v, 1, 0)
        w = pltpu.roll(v, n_ - 2, 0) - pltpu.roll(v, 2, 0)
        return (8.0 * g - w) * third

    def shrink(v, margin, keep):
        size = v.shape[0]
        cut = margin - keep
        line = lax.broadcasted_iota(jnp.int32, v.shape, 0)
        moved = jnp.where(line < rows + keep, v, pltpu.roll(v, size - 2 * cut, 0))
        return moved[: size - 2 * cut]

    def tend(h, e, n):
        depth = 4.0 + h
        ch = -(dx(depth * e) + dy(depth * n))
        ce = -(e * dx(e) + n * dy(e)) + f * n - dx(h)
        cn = -(e * dx(n) + n * dy(n)) - f * e - dy(h)
        return ch, ce, cn

    s = (ring[0], ring[1], ring[2])
    margin = (R - rows) // 2
    for step in range(steps):
        keep = 4 * (steps - step)
        if keep < margin and (rows + 2 * keep) % 8 == 0:
            s = tuple(shrink(v, margin, keep) for v in s)
            f = shrink(f, margin, keep)
            margin = keep
        first = tend(*s)
        mid = tuple(a + 0.1 * b for a, b in zip(s, first))
        second = tend(*mid)
        s = tuple(a + 0.05 * (b + c) for a, b, c in zip(s, first, second))
    for k in range(3):
        o_ref[0, k] = s[k][:rows, :cols]


def forecast(cor, value, above, below, west, east, steps):
    S, F, rows, cols = value.shape
    R, C = cor.shape
    width = above.shape[-2]
    return pl.pallas_call(
        functools.partial(forecast_kernel, steps=steps),
        out_shape=jax.ShapeDtypeStruct((S, F, rows, cols), jnp.float32),
        grid=(S,),
        in_specs=[
            pl.BlockSpec((R, C), lambda i: (0, 0)),
            pl.BlockSpec((1, F, rows, cols), lambda i: (i, 0, 0, 0)),
            pl.BlockSpec((1, F, width, cols), lambda i: (i, 0, 0, 0)),
            pl.BlockSpec((1, F, width, cols), lambda i: (i, 0, 0, 0)),
            pl.BlockSpec((1, F, R, width), lambda i: (i, 0, 0, 0)),
            pl.BlockSpec((1, F, R, width), lambda i: (i, 0, 0, 0)),
        ],
        out_specs=pl.BlockSpec((1, F, rows, cols), lambda i: (i, 0, 0, 0)),
        scratch_shapes=[
            pltpu.VMEM((F, R, C), jnp.float32),
            pltpu.VMEM((R, C - cols), jnp.float32),
            pltpu.VMEM((R, C - cols), jnp.float32),
        ],
        cost_estimate=pl.CostEstimate(
            flops=S * F * R * C * 300 * steps, transcendentals=0, bytes_accessed=4 * S * F * (R * C + rows * cols)
        ),
    )(cor, value, above, below, west, east)


def body(control, perts):
    tile_rows, tile_column_count = (control.shape[1], control.shape[2])
    grid_rows = tile_rows * lax.axis_size("gy")
    grid_cols = tile_column_count * lax.axis_size("gx")
    first_row = lax.axis_index("gy") * tile_rows
    margin = 4 * STEPS
    lanes = 128 * (-(-(tile_column_count + 2 * margin) // 128))
    ring_rows = tile_rows + 2 * margin
    offsets = jnp.arange(ring_rows, dtype=jnp.int32)
    offsets = jnp.where(offsets < tile_rows + margin, offsets, offsets - ring_rows)
    rows = ((first_row + offsets) % grid_rows).astype(jnp.float32)
    coriolis = coriolis_mid * (1.0 + 0.5 * jnp.sin(two_pi * rows / float(grid_rows)))
    coriolis = jnp.broadcast_to(coriolis[:, None], (ring_rows, lanes))

    states = jnp.concatenate([control[None], control[None] + perts], 0)
    above, below, west, east = ring_halo(states, margin, lanes)
    current = forecast(coriolis, states, above, below, west, east, STEPS)
    bred = current[1:] - current[0:1]
    flat = bred.reshape(MEMBERS, -1)
    local_gram = jnp.dot(flat, flat.T, precision=lax.Precision.HIGHEST)
    gram = local_gram
    for axis in ("gx", "gy"):
        count = lax.axis_size(axis)
        if count & (count - 1):
            gram = lax.psum(gram, axis)
            continue
        stride = 1
        while stride < count:
            pairs = [(i, i ^ stride) for i in range(count)]
            gram = gram + lax.ppermute(gram, axis, pairs)
            stride *= 2
    lower = jnp.linalg.cholesky(gram)
    solved = jax.scipy.linalg.solve_triangular(lower, flat, lower=True)
    domain_length = 3 * grid_rows * grid_cols
    basis = (math.sqrt(domain_length) * solved).reshape(perts.shape)
    rfactor = lower.T / math.sqrt(domain_length)
    return (basis, rfactor)


def solution(mesh):
    in_specs = (P(None, "gy", "gx"), P(None, None, "gy", "gx"))
    out_specs = (P(None, None, "gy", "gx"), P())
    return jax.shard_map(body, mesh=mesh, in_specs=in_specs, out_specs=out_specs, check_vma=False)
```

```python
import functools
import math

import jax
import jax.numpy as jnp
from jax import lax
from jax.experimental import pallas as pl
from jax.experimental.pallas import tpu as pltpu
from jax.sharding import PartitionSpec as P

MEMBERS = 16
STEPS = 2


mean_depth = 4.0
gravity = 1.0
coriolis_mid = 0.5
time_step = 0.1
two_pi = 2.0 * math.pi


def ring_halo(value, width, lanes):
    rows, cols = (value.shape[-2], value.shape[-1])
    across, down = (lax.axis_size("gx"), lax.axis_size("gy"))

    def shift(part, axes, dx, dy, flatten=True):
        pairs = []
        for x in range(across):
            for y in range(down):
                target = ((x + dx) % across, (y + dy) % down)
                if axes == "gx":
                    pairs.append((x, target[0])) if y == 0 else None
                elif axes == "gy":
                    pairs.append((y, target[1])) if x == 0 else None
                else:
                    pairs.append((x * down + y, target[0] * down + target[1]))
        if not flatten:
            return lax.ppermute(part, axes, pairs)
        flat = part.reshape(-1)
        return lax.ppermute(flat, axes, pairs).reshape(part.shape)

    top, bottom = (value[..., :width, :], value[..., rows - width :, :])
    above = shift(bottom, "gy", 0, 1, flatten=False)
    below = shift(top, "gy", 0, -1, flatten=False)
    tall = jnp.concatenate([value, below, above], axis=-2)
    west = shift(tall[..., cols - width :], "gx", 1, 0)
    east = shift(tall[..., :width], "gx", -1, 0)
    return above, below, west, east


def forecast_kernel(cor_ref, x_ref, up_ref, down_ref, west_ref, east_ref, o_ref, ring, east_pad, west_pad, *, steps):
    rows, cols = (x_ref.shape[-2], x_ref.shape[-1])
    R, C = cor_ref.shape
    width = up_ref.shape[-2]
    spare = C - cols

    @pl.when(pl.program_id(0) == 0)
    def _():
        ring[...] = jnp.zeros_like(ring)
        east_pad[...] = jnp.zeros_like(east_pad)
        west_pad[...] = jnp.zeros_like(west_pad)

    base = cor_ref[...]
    third = 1.0 / 12.0

    def dx(v):
        n_ = v.shape[1]
        g = pltpu.roll(v, n_ - 1, 1) - pltpu.roll(v, 1, 1)
        w = pltpu.roll(v, n_ - 2, 1) - pltpu.roll(v, 2, 1)
        return (8.0 * g - w) * third

    def dy(v):
        n_ = v.shape[0]
        g = pltpu.roll(v, n_ - 1, 0) - pltpu.roll(v, 1, 0)
        w = pltpu.roll(v, n_ - 2, 0) - pltpu.roll(v, 2, 0)
        return (8.0 * g - w) * third

    def shrink(v, margin, keep):
        size = v.shape[0]
        cut = margin - keep
        line = lax.broadcasted_iota(jnp.int32, v.shape, 0)
        moved = jnp.where(line < rows + keep, v, pltpu.roll(v, size - 2 * cut, 0))
        return moved[: size - 2 * cut]

    def tend(h, e, n, f):
        depth = 4.0 + h
        ch = -(dx(depth * e) + dy(depth * n))
        ce = -(e * dx(e) + n * dy(e)) + f * n - dx(h)
        cn = -(e * dx(n) + n * dy(n)) - f * e - dy(h)
        return ch, ce, cn

    def one(i, carry):
        for k in range(3):
            ring[k, :rows, :cols] = x_ref[i, k]
            ring[k, rows : rows + width, :cols] = down_ref[i, k]
            ring[k, rows + width :, :cols] = up_ref[i, k]
            east_pad[:, :width] = east_ref[i, k]
            west_pad[:, :width] = west_ref[i, k]
            ring[k, :, cols:] = east_pad[...] + pltpu.roll(west_pad[...], spare - width, 1)

        f = base
        s = (ring[0], ring[1], ring[2])
        margin = (R - rows) // 2
        for step in range(steps):
            keep = 4 * (steps - step)
            if keep < margin and (rows + 2 * keep) % 8 == 0:
                s = tuple(shrink(v, margin, keep) for v in s)
                f = shrink(f, margin, keep)
                margin = keep
            first = tend(*s, f)
            mid = tuple(a + 0.1 * b for a, b in zip(s, first))
            second = tend(*mid, f)
            s = tuple(a + 0.05 * (b + c) for a, b, c in zip(s, first, second))
        for k in range(3):
            o_ref[i, k] = s[k][:rows, :cols]

        return carry

    lax.fori_loop(0, x_ref.shape[0], one, 0)


def forecast(cor, value, above, below, west, east, steps):
    S, F, rows, cols = value.shape
    R, C = cor.shape
    width = above.shape[-2]
    return pl.pallas_call(
        functools.partial(forecast_kernel, steps=steps),
        out_shape=jax.ShapeDtypeStruct((S, F, rows, cols), jnp.float32),
        grid=(1,),
        in_specs=[
            pl.BlockSpec((R, C), lambda i: (0, 0), pipeline_mode=pl.Buffered(1)),
            pl.BlockSpec((S, F, rows, cols), lambda i: (0, 0, 0, 0), pipeline_mode=pl.Buffered(1)),
            pl.BlockSpec((S, F, width, cols), lambda i: (0, 0, 0, 0), pipeline_mode=pl.Buffered(1)),
            pl.BlockSpec((S, F, width, cols), lambda i: (0, 0, 0, 0), pipeline_mode=pl.Buffered(1)),
            pl.BlockSpec((S, F, R, width), lambda i: (0, 0, 0, 0), pipeline_mode=pl.Buffered(1)),
            pl.BlockSpec((S, F, R, width), lambda i: (0, 0, 0, 0), pipeline_mode=pl.Buffered(1)),
        ],
        out_specs=pl.BlockSpec((S, F, rows, cols), lambda i: (0, 0, 0, 0), pipeline_mode=pl.Buffered(1)),
        scratch_shapes=[
            pltpu.VMEM((F, R, C), jnp.float32),
            pltpu.VMEM((R, C - cols), jnp.float32),
            pltpu.VMEM((R, C - cols), jnp.float32),
        ],
        cost_estimate=pl.CostEstimate(
            flops=S * F * R * C * 300 * steps, transcendentals=0, bytes_accessed=4 * S * F * (R * C + rows * cols)
        ),
    )(cor, value, above, below, west, east)


def body(control, perts):
    tile_rows, tile_column_count = (control.shape[1], control.shape[2])
    grid_rows = tile_rows * lax.axis_size("gy")
    grid_cols = tile_column_count * lax.axis_size("gx")
    first_row = lax.axis_index("gy") * tile_rows
    margin = 4 * STEPS
    lanes = 128 * (-(-(tile_column_count + 2 * margin) // 128))
    ring_rows = tile_rows + 2 * margin
    offsets = jnp.arange(ring_rows, dtype=jnp.int32)
    offsets = jnp.where(offsets < tile_rows + margin, offsets, offsets - ring_rows)
    rows = ((first_row + offsets) % grid_rows).astype(jnp.float32)
    coriolis = coriolis_mid * (1.0 + 0.5 * jnp.sin(two_pi * rows / float(grid_rows)))
    coriolis = jnp.broadcast_to(coriolis[:, None], (ring_rows, lanes))

    states = jnp.concatenate([control[None], control[None] + perts], 0)
    above, below, west, east = ring_halo(states, margin, lanes)
    current = forecast(coriolis, states, above, below, west, east, STEPS)
    bred = current[1:] - current[0:1]
    flat = bred.reshape(MEMBERS, -1)
    local_gram = jnp.dot(flat, flat.T, precision=lax.Precision.HIGHEST)
    gram = local_gram
    for axis in ("gx", "gy"):
        count = lax.axis_size(axis)
        if count & (count - 1):
            gram = lax.psum(gram, axis)
            continue
        stride = 1
        while stride < count:
            pairs = [(i, i ^ stride) for i in range(count)]
            gram = gram + lax.ppermute(gram, axis, pairs)
            stride *= 2
    lower = jnp.linalg.cholesky(gram)
    solved = jax.scipy.linalg.solve_triangular(lower, flat, lower=True)
    domain_length = 3 * grid_rows * grid_cols
    basis = (math.sqrt(domain_length) * solved).reshape(perts.shape)
    rfactor = lower.T / math.sqrt(domain_length)
    return (basis, rfactor)


def solution(mesh):
    in_specs = (P(None, "gy", "gx"), P(None, None, "gy", "gx"))
    out_specs = (P(None, None, "gy", "gx"), P())
    return jax.shard_map(body, mesh=mesh, in_specs=in_specs, out_specs=out_specs, check_vma=False)
```

```python
import functools
import math

import jax
import jax.numpy as jnp
from jax import lax
from jax.experimental import pallas as pl
from jax.experimental.pallas import tpu as pltpu
from jax.sharding import PartitionSpec as P

MEMBERS = 16
STEPS = 2


mean_depth = 4.0
gravity = 1.0
coriolis_mid = 0.5
time_step = 0.1
two_pi = 2.0 * math.pi


def ring_halo(value, width, lanes):
    rows, cols = (value.shape[-2], value.shape[-1])
    across, down = (lax.axis_size("gx"), lax.axis_size("gy"))

    def shift(part, axes, dx, dy, flatten=True):
        pairs = []
        for x in range(across):
            for y in range(down):
                target = ((x + dx) % across, (y + dy) % down)
                if axes == "gx":
                    pairs.append((x, target[0])) if y == 0 else None
                elif axes == "gy":
                    pairs.append((y, target[1])) if x == 0 else None
                else:
                    pairs.append((x * down + y, target[0] * down + target[1]))
        if not flatten:
            return lax.ppermute(part, axes, pairs)
        flat = part.reshape(-1)
        return lax.ppermute(flat, axes, pairs).reshape(part.shape)

    top, bottom = (value[..., :width, :], value[..., rows - width :, :])
    above = shift(bottom, "gy", 0, 1, flatten=False)
    below = shift(top, "gy", 0, -1, flatten=False)
    tall = jnp.concatenate([above, value, below], axis=-2)
    west = shift(tall[..., cols - width :], "gx", 1, 0)
    east = shift(tall[..., :width], "gx", -1, 0)
    return above, below, west, east


def forecast_kernel(cor_ref, x_ref, up_ref, down_ref, west_ref, east_ref, o_ref, ring, east_pad, west_pad, shifted, *, steps):
    rows, cols = (x_ref.shape[-2], x_ref.shape[-1])
    R, C = cor_ref.shape
    width = up_ref.shape[-2]
    spare = C - cols

    @pl.when(pl.program_id(0) == 0)
    def _():
        ring[...] = jnp.zeros_like(ring)
        east_pad[...] = jnp.zeros_like(east_pad)
        west_pad[...] = jnp.zeros_like(west_pad)
        shifted[...] = jnp.zeros_like(shifted)

    for k in range(3):
        ring[k, :width, :cols] = up_ref[0, k]
        ring[k, width : width + rows, :cols] = x_ref[0, k]
        ring[k, width + rows :, :cols] = down_ref[0, k]
        east_pad[:, :width] = east_ref[0, k]
        west_pad[:, :width] = west_ref[0, k]
        ring[k, :, cols:] = east_pad[...] + pltpu.roll(west_pad[...], spare - width, 1)

    f = cor_ref[...]
    third = 1.0 / 12.0

    def dx(v):
        g = pltpu.roll(v, C - 1, 1) - pltpu.roll(v, 1, 1)
        w = pltpu.roll(v, C - 2, 1) - pltpu.roll(v, 2, 1)
        return (8.0 * g - w) * third

    def dy(v):
        shifted[8 : 8 + R, :] = v
        g = shifted[pl.ds(9, R), :] - shifted[pl.ds(7, R), :]
        w = shifted[pl.ds(10, R), :] - shifted[pl.ds(6, R), :]
        return (8.0 * g - w) * third

    def tend(h, e, n):
        depth = 4.0 + h
        ch = -(dx(depth * e) + dy(depth * n))
        ce = -(e * dx(e) + n * dy(e)) + f * n - dx(h)
        cn = -(e * dx(n) + n * dy(n)) - f * e - dy(h)
        return ch, ce, cn

    s = (ring[0], ring[1], ring[2])
    for _ in range(steps):
        first = tend(*s)
        mid = tuple(a + 0.1 * b for a, b in zip(s, first))
        second = tend(*mid)
        s = tuple(a + 0.05 * (b + c) for a, b, c in zip(s, first, second))
    for k in range(3):
        o_ref[0, k] = s[k][width : width + rows, :cols]


def forecast(cor, value, above, below, west, east, steps):
    S, F, rows, cols = value.shape
    R, C = cor.shape
    width = above.shape[-2]
    return pl.pallas_call(
        functools.partial(forecast_kernel, steps=steps),
        out_shape=jax.ShapeDtypeStruct((S, F, rows, cols), jnp.float32),
        grid=(S,),
        in_specs=[
            pl.BlockSpec((R, C), lambda i: (0, 0)),
            pl.BlockSpec((1, F, rows, cols), lambda i: (i, 0, 0, 0)),
            pl.BlockSpec((1, F, width, cols), lambda i: (i, 0, 0, 0)),
            pl.BlockSpec((1, F, width, cols), lambda i: (i, 0, 0, 0)),
            pl.BlockSpec((1, F, R, width), lambda i: (i, 0, 0, 0)),
            pl.BlockSpec((1, F, R, width), lambda i: (i, 0, 0, 0)),
        ],
        out_specs=pl.BlockSpec((1, F, rows, cols), lambda i: (i, 0, 0, 0)),
        scratch_shapes=[
            pltpu.VMEM((F, R, C), jnp.float32),
            pltpu.VMEM((R, C - cols), jnp.float32),
            pltpu.VMEM((R, C - cols), jnp.float32),
            pltpu.VMEM((R + 16, C), jnp.float32),
        ],
        cost_estimate=pl.CostEstimate(
            flops=S * F * R * C * 300 * steps, transcendentals=0, bytes_accessed=4 * S * F * (R * C + rows * cols)
        ),
    )(cor, value, above, below, west, east)


def body(control, perts):
    tile_rows, tile_column_count = (control.shape[1], control.shape[2])
    grid_rows = tile_rows * lax.axis_size("gy")
    grid_cols = tile_column_count * lax.axis_size("gx")
    first_row = lax.axis_index("gy") * tile_rows
    margin = 4 * STEPS
    lanes = 128 * (-(-(tile_column_count + 2 * margin) // 128))
    ring_rows = tile_rows + 2 * margin
    offsets = jnp.arange(ring_rows, dtype=jnp.int32) - margin
    rows = ((first_row + offsets) % grid_rows).astype(jnp.float32)
    coriolis = coriolis_mid * (1.0 + 0.5 * jnp.sin(two_pi * rows / float(grid_rows)))
    coriolis = jnp.broadcast_to(coriolis[:, None], (ring_rows, lanes))

    states = jnp.concatenate([control[None], control[None] + perts], 0)
    above, below, west, east = ring_halo(states, margin, lanes)
    current = forecast(coriolis, states, above, below, west, east, STEPS)
    bred = current[1:] - current[0:1]
    flat = bred.reshape(MEMBERS, -1)
    local_gram = jnp.dot(flat, flat.T, precision=lax.Precision.HIGHEST)
    gram = local_gram
    for axis in ("gx", "gy"):
        count = lax.axis_size(axis)
        if count & (count - 1):
            gram = lax.psum(gram, axis)
            continue
        stride = 1
        while stride < count:
            pairs = [(i, i ^ stride) for i in range(count)]
            gram = gram + lax.ppermute(gram, axis, pairs)
            stride *= 2
    lower = jnp.linalg.cholesky(gram)
    solved = jax.scipy.linalg.solve_triangular(lower, flat, lower=True)
    domain_length = 3 * grid_rows * grid_cols
    basis = (math.sqrt(domain_length) * solved).reshape(perts.shape)
    rfactor = lower.T / math.sqrt(domain_length)
    return (basis, rfactor)


def solution(mesh):
    in_specs = (P(None, "gy", "gx"), P(None, None, "gy", "gx"))
    out_specs = (P(None, None, "gy", "gx"), P())
    return jax.shard_map(body, mesh=mesh, in_specs=in_specs, out_specs=out_specs, check_vma=False)
```

```python
import functools
import math

import jax
import jax.numpy as jnp
from jax import lax
from jax.experimental import pallas as pl
from jax.experimental.pallas import tpu as pltpu
from jax.sharding import PartitionSpec as P

MEMBERS = 16
STEPS = 2


mean_depth = 4.0
gravity = 1.0
coriolis_mid = 0.5
time_step = 0.1
two_pi = 2.0 * math.pi


def ring_halo(value, width, lanes):
    rows, cols = (value.shape[-2], value.shape[-1])
    across, down = (lax.axis_size("gx"), lax.axis_size("gy"))

    def shift(part, axes, dx, dy, flatten=True):
        pairs = []
        for x in range(across):
            for y in range(down):
                target = ((x + dx) % across, (y + dy) % down)
                if axes == "gx":
                    pairs.append((x, target[0])) if y == 0 else None
                elif axes == "gy":
                    pairs.append((y, target[1])) if x == 0 else None
                else:
                    pairs.append((x * down + y, target[0] * down + target[1]))
        if not flatten:
            return lax.ppermute(part, axes, pairs)
        flat = part.reshape(-1)
        return lax.ppermute(flat, axes, pairs).reshape(part.shape)

    top, bottom = (value[..., :width, :], value[..., rows - width :, :])
    above = shift(bottom, "gy", 0, 1, flatten=False)
    below = shift(top, "gy", 0, -1, flatten=False)
    tall = jnp.concatenate([value, below, above], axis=-2)
    west = shift(tall[..., cols - width :], "gx", 1, 0)
    east = shift(tall[..., :width], "gx", -1, 0)
    return above, below, west, east


def forecast_kernel(cor_ref, c_ref, p_ref, up_ref, down_ref, west_ref, east_ref, o_ref, ring, east_pad, west_pad, *, steps):
    rows, cols = (c_ref.shape[-2], c_ref.shape[-1])
    state = pl.program_id(0)
    R, C = cor_ref.shape
    width = up_ref.shape[-2]
    spare = C - cols

    @pl.when(pl.program_id(0) == 0)
    def _():
        ring[...] = jnp.zeros_like(ring)
        east_pad[...] = jnp.zeros_like(east_pad)
        west_pad[...] = jnp.zeros_like(west_pad)

    @pl.when(state == 0)
    def _():
        for k in range(3):
            ring[k, :rows, :cols] = c_ref[k]

    @pl.when(state > 0)
    def _():
        for k in range(3):
            ring[k, :rows, :cols] = c_ref[k] + p_ref[0, k]

    for k in range(3):
        ring[k, rows : rows + width, :cols] = down_ref[0, k]
        ring[k, rows + width :, :cols] = up_ref[0, k]
        east_pad[:, :width] = east_ref[0, k]
        west_pad[:, :width] = west_ref[0, k]
        ring[k, :, cols:] = east_pad[...] + pltpu.roll(west_pad[...], spare - width, 1)

    f = cor_ref[...]
    third = 1.0 / 12.0

    def dx(v):
        n_ = v.shape[1]
        g = pltpu.roll(v, n_ - 1, 1) - pltpu.roll(v, 1, 1)
        w = pltpu.roll(v, n_ - 2, 1) - pltpu.roll(v, 2, 1)
        return (8.0 * g - w) * third

    def dy(v):
        n_ = v.shape[0]
        g = pltpu.roll(v, n_ - 1, 0) - pltpu.roll(v, 1, 0)
        w = pltpu.roll(v, n_ - 2, 0) - pltpu.roll(v, 2, 0)
        return (8.0 * g - w) * third

    def shrink(v, margin, keep):
        size = v.shape[0]
        cut = margin - keep
        line = lax.broadcasted_iota(jnp.int32, v.shape, 0)
        moved = jnp.where(line < rows + keep, v, pltpu.roll(v, size - 2 * cut, 0))
        return moved[: size - 2 * cut]

    def tend(h, e, n):
        depth = 4.0 + h
        ch = -(dx(depth * e) + dy(depth * n))
        ce = -(e * dx(e) + n * dy(e)) + f * n - dx(h)
        cn = -(e * dx(n) + n * dy(n)) - f * e - dy(h)
        return ch, ce, cn

    s = (ring[0], ring[1], ring[2])
    margin = (R - rows) // 2
    for step in range(steps):
        keep = 4 * (steps - step)
        if keep < margin and (rows + 2 * keep) % 8 == 0:
            s = tuple(shrink(v, margin, keep) for v in s)
            f = shrink(f, margin, keep)
            margin = keep
        first = tend(*s)
        mid = tuple(a + 0.1 * b for a, b in zip(s, first))
        second = tend(*mid)
        s = tuple(a + 0.05 * (b + c) for a, b, c in zip(s, first, second))
    for k in range(3):
        o_ref[0, k] = s[k][:rows, :cols]


def forecast(cor, control, perts, above, below, west, east, steps):
    F, rows, cols = control.shape
    S = perts.shape[0] + 1
    R, C = cor.shape
    width = above.shape[-2]
    return pl.pallas_call(
        functools.partial(forecast_kernel, steps=steps),
        out_shape=jax.ShapeDtypeStruct((S, F, rows, cols), jnp.float32),
        grid=(S,),
        in_specs=[
            pl.BlockSpec((R, C), lambda i: (0, 0)),
            pl.BlockSpec((F, rows, cols), lambda i: (0, 0, 0)),
            pl.BlockSpec((1, F, rows, cols), lambda i: (jnp.maximum(i - 1, 0), 0, 0, 0)),
            pl.BlockSpec((1, F, width, cols), lambda i: (i, 0, 0, 0)),
            pl.BlockSpec((1, F, width, cols), lambda i: (i, 0, 0, 0)),
            pl.BlockSpec((1, F, R, width), lambda i: (i, 0, 0, 0)),
            pl.BlockSpec((1, F, R, width), lambda i: (i, 0, 0, 0)),
        ],
        out_specs=pl.BlockSpec((1, F, rows, cols), lambda i: (i, 0, 0, 0)),
        scratch_shapes=[
            pltpu.VMEM((F, R, C), jnp.float32),
            pltpu.VMEM((R, C - cols), jnp.float32),
            pltpu.VMEM((R, C - cols), jnp.float32),
        ],
        cost_estimate=pl.CostEstimate(
            flops=S * F * R * C * 300 * steps, transcendentals=0, bytes_accessed=4 * S * F * (R * C + rows * cols)
        ),
    )(cor, control, perts, above, below, west, east)


def body(control, perts):
    tile_rows, tile_column_count = (control.shape[1], control.shape[2])
    grid_rows = tile_rows * lax.axis_size("gy")
    grid_cols = tile_column_count * lax.axis_size("gx")
    first_row = lax.axis_index("gy") * tile_rows
    margin = 4 * STEPS
    lanes = 128 * (-(-(tile_column_count + 2 * margin) // 128))
    ring_rows = tile_rows + 2 * margin
    offsets = jnp.arange(ring_rows, dtype=jnp.int32)
    offsets = jnp.where(offsets < tile_rows + margin, offsets, offsets - ring_rows)
    rows = ((first_row + offsets) % grid_rows).astype(jnp.float32)
    coriolis = coriolis_mid * (1.0 + 0.5 * jnp.sin(two_pi * rows / float(grid_rows)))
    coriolis = jnp.broadcast_to(coriolis[:, None], (ring_rows, lanes))

    states = jnp.concatenate([control[None], control[None] + perts], 0)
    above, below, west, east = ring_halo(states, margin, lanes)
    current = forecast(coriolis, control, perts, above, below, west, east, STEPS)
    bred = current[1:] - current[0:1]
    flat = bred.reshape(MEMBERS, -1)
    local_gram = jnp.dot(flat, flat.T, precision=lax.Precision.HIGHEST)
    gram = local_gram
    for axis in ("gx", "gy"):
        count = lax.axis_size(axis)
        if count & (count - 1):
            gram = lax.psum(gram, axis)
            continue
        stride = 1
        while stride < count:
            pairs = [(i, i ^ stride) for i in range(count)]
            gram = gram + lax.ppermute(gram, axis, pairs)
            stride *= 2
    lower = jnp.linalg.cholesky(gram)
    solved = jax.scipy.linalg.solve_triangular(lower, flat, lower=True)
    domain_length = 3 * grid_rows * grid_cols
    basis = (math.sqrt(domain_length) * solved).reshape(perts.shape)
    rfactor = lower.T / math.sqrt(domain_length)
    return (basis, rfactor)


def solution(mesh):
    in_specs = (P(None, "gy", "gx"), P(None, None, "gy", "gx"))
    out_specs = (P(None, None, "gy", "gx"), P())
    return jax.shard_map(body, mesh=mesh, in_specs=in_specs, out_specs=out_specs, check_vma=False)
```

```python
import functools
import math

import jax
import jax.numpy as jnp
from jax import lax
from jax.experimental import pallas as pl
from jax.experimental.pallas import tpu as pltpu
from jax.sharding import PartitionSpec as P

MEMBERS = 16
STEPS = 2


mean_depth = 4.0
gravity = 1.0
coriolis_mid = 0.5
time_step = 0.1
two_pi = 2.0 * math.pi


def shift(part, axes, dx, dy, flatten=True):
    across, down = (lax.axis_size("gx"), lax.axis_size("gy"))
    pairs = []
    for x in range(across):
        for y in range(down):
            target = ((x + dx) % across, (y + dy) % down)
            if axes == "gx":
                pairs.append((x, target[0])) if y == 0 else None
            else:
                pairs.append((y, target[1])) if x == 0 else None
    if not flatten:
        return lax.ppermute(part, axes, pairs)
    flat = part.reshape(-1)
    return lax.ppermute(flat, axes, pairs).reshape(part.shape)


def ring_halo(control, perts, width):
    rows, cols = (control.shape[-2], control.shape[-1])

    def part(index):
        base = control[None][index]
        return jnp.concatenate([base, base + perts[index]], 0)

    top = part((Ellipsis, slice(0, width), slice(None)))
    bottom = part((Ellipsis, slice(rows - width, rows), slice(None)))
    left = part((Ellipsis, slice(None), slice(0, width)))
    right = part((Ellipsis, slice(None), slice(cols - width, cols)))
    above = shift(bottom, "gy", 0, 1, flatten=False)
    below = shift(top, "gy", 0, -1, flatten=False)
    west_source = jnp.concatenate([right, below[..., cols - width :], above[..., cols - width :]], axis=-2)
    east_source = jnp.concatenate([left, below[..., :width], above[..., :width]], axis=-2)
    west = shift(west_source, "gx", 1, 0)
    east = shift(east_source, "gx", -1, 0)
    return above, below, west, east


def forecast_kernel(cor_ref, c_ref, p_ref, up_ref, down_ref, west_ref, east_ref, o_ref, ring, east_pad, west_pad, *, steps):
    rows, cols = (c_ref.shape[-2], c_ref.shape[-1])
    state = pl.program_id(0)
    R, C = cor_ref.shape
    width = up_ref.shape[-2]
    spare = C - cols

    @pl.when(pl.program_id(0) == 0)
    def _():
        ring[...] = jnp.zeros_like(ring)
        east_pad[...] = jnp.zeros_like(east_pad)
        west_pad[...] = jnp.zeros_like(west_pad)

    @pl.when(state == 0)
    def _():
        for k in range(3):
            ring[k, :rows, :cols] = c_ref[k]

    @pl.when(state > 0)
    def _():
        for k in range(3):
            ring[k, :rows, :cols] = c_ref[k] + p_ref[0, k]

    for k in range(3):
        ring[k, rows : rows + width, :cols] = down_ref[0, k]
        ring[k, rows + width :, :cols] = up_ref[0, k]
        east_pad[:, :width] = east_ref[0, k]
        west_pad[:, :width] = west_ref[0, k]
        ring[k, :, cols:] = east_pad[...] + pltpu.roll(west_pad[...], spare - width, 1)

    f = cor_ref[...]
    third = 1.0 / 12.0

    def dx(v):
        n_ = v.shape[1]
        g = pltpu.roll(v, n_ - 1, 1) - pltpu.roll(v, 1, 1)
        w = pltpu.roll(v, n_ - 2, 1) - pltpu.roll(v, 2, 1)
        return (8.0 * g - w) * third

    def dy(v):
        n_ = v.shape[0]
        g = pltpu.roll(v, n_ - 1, 0) - pltpu.roll(v, 1, 0)
        w = pltpu.roll(v, n_ - 2, 0) - pltpu.roll(v, 2, 0)
        return (8.0 * g - w) * third

    def shrink(v, margin, keep):
        size = v.shape[0]
        cut = margin - keep
        line = lax.broadcasted_iota(jnp.int32, v.shape, 0)
        moved = jnp.where(line < rows + keep, v, pltpu.roll(v, size - 2 * cut, 0))
        return moved[: size - 2 * cut]

    def tend(h, e, n):
        depth = 4.0 + h
        ch = -(dx(depth * e) + dy(depth * n))
        ce = -(e * dx(e) + n * dy(e)) + f * n - dx(h)
        cn = -(e * dx(n) + n * dy(n)) - f * e - dy(h)
        return ch, ce, cn

    s = (ring[0], ring[1], ring[2])
    margin = (R - rows) // 2
    for step in range(steps):
        keep = 4 * (steps - step)
        if keep < margin and (rows + 2 * keep) % 8 == 0:
            s = tuple(shrink(v, margin, keep) for v in s)
            f = shrink(f, margin, keep)
            margin = keep
        first = tend(*s)
        mid = tuple(a + 0.1 * b for a, b in zip(s, first))
        second = tend(*mid)
        s = tuple(a + 0.05 * (b + c) for a, b, c in zip(s, first, second))
    for k in range(3):
        o_ref[0, k] = s[k][:rows, :cols]


def forecast(cor, control, perts, above, below, west, east, steps):
    F, rows, cols = control.shape
    S = perts.shape[0] + 1
    R, C = cor.shape
    width = above.shape[-2]
    return pl.pallas_call(
        functools.partial(forecast_kernel, steps=steps),
        out_shape=jax.ShapeDtypeStruct((S, F, rows, cols), jnp.float32),
        grid=(S,),
        in_specs=[
            pl.BlockSpec((R, C), lambda i: (0, 0)),
            pl.BlockSpec((F, rows, cols), lambda i: (0, 0, 0)),
            pl.BlockSpec((1, F, rows, cols), lambda i: (jnp.maximum(i - 1, 0), 0, 0, 0)),
            pl.BlockSpec((1, F, width, cols), lambda i: (i, 0, 0, 0)),
            pl.BlockSpec((1, F, width, cols), lambda i: (i, 0, 0, 0)),
            pl.BlockSpec((1, F, R, width), lambda i: (i, 0, 0, 0)),
            pl.BlockSpec((1, F, R, width), lambda i: (i, 0, 0, 0)),
        ],
        out_specs=pl.BlockSpec((1, F, rows, cols), lambda i: (i, 0, 0, 0)),
        scratch_shapes=[
            pltpu.VMEM((F, R, C), jnp.float32),
            pltpu.VMEM((R, C - cols), jnp.float32),
            pltpu.VMEM((R, C - cols), jnp.float32),
        ],
        cost_estimate=pl.CostEstimate(
            flops=S * F * R * C * 300 * steps, transcendentals=0, bytes_accessed=4 * S * F * (R * C + rows * cols)
        ),
    )(cor, control, perts, above, below, west, east)


def body(control, perts):
    tile_rows, tile_column_count = (control.shape[1], control.shape[2])
    grid_rows = tile_rows * lax.axis_size("gy")
    grid_cols = tile_column_count * lax.axis_size("gx")
    first_row = lax.axis_index("gy") * tile_rows
    margin = 4 * STEPS
    lanes = 128 * (-(-(tile_column_count + 2 * margin) // 128))
    ring_rows = tile_rows + 2 * margin
    offsets = jnp.arange(ring_rows, dtype=jnp.int32)
    offsets = jnp.where(offsets < tile_rows + margin, offsets, offsets - ring_rows)
    rows = ((first_row + offsets) % grid_rows).astype(jnp.float32)
    coriolis = coriolis_mid * (1.0 + 0.5 * jnp.sin(two_pi * rows / float(grid_rows)))
    coriolis = jnp.broadcast_to(coriolis[:, None], (ring_rows, lanes))

    above, below, west, east = ring_halo(control, perts, margin)
    current = forecast(coriolis, control, perts, above, below, west, east, STEPS)
    bred = current[1:] - current[0:1]
    flat = bred.reshape(MEMBERS, -1)
    local_gram = jnp.dot(flat, flat.T, precision=lax.Precision.HIGHEST)
    gram = local_gram
    for axis in ("gx", "gy"):
        count = lax.axis_size(axis)
        if count & (count - 1):
            gram = lax.psum(gram, axis)
            continue
        stride = 1
        while stride < count:
            pairs = [(i, i ^ stride) for i in range(count)]
            gram = gram + lax.ppermute(gram, axis, pairs)
            stride *= 2
    lower = jnp.linalg.cholesky(gram)
    solved = jax.scipy.linalg.solve_triangular(lower, flat, lower=True)
    domain_length = 3 * grid_rows * grid_cols
    basis = (math.sqrt(domain_length) * solved).reshape(perts.shape)
    rfactor = lower.T / math.sqrt(domain_length)
    return (basis, rfactor)


def solution(mesh):
    in_specs = (P(None, "gy", "gx"), P(None, None, "gy", "gx"))
    out_specs = (P(None, None, "gy", "gx"), P())
    return jax.shard_map(body, mesh=mesh, in_specs=in_specs, out_specs=out_specs, check_vma=False)
```

```python
import functools
import math

import jax
import jax.numpy as jnp
from jax import lax
from jax.experimental import pallas as pl
from jax.experimental.pallas import tpu as pltpu
from jax.sharding import PartitionSpec as P

MEMBERS = 16
STEPS = 2


mean_depth = 4.0
gravity = 1.0
coriolis_mid = 0.5
time_step = 0.1
two_pi = 2.0 * math.pi


def ring_halo(value, width, lanes):
    rows, cols = (value.shape[-2], value.shape[-1])
    across, down = (lax.axis_size("gx"), lax.axis_size("gy"))

    def shift(part, axes, dx, dy, flatten=True):
        pairs = []
        for x in range(across):
            for y in range(down):
                target = ((x + dx) % across, (y + dy) % down)
                if axes == "gx":
                    pairs.append((x, target[0])) if y == 0 else None
                elif axes == "gy":
                    pairs.append((y, target[1])) if x == 0 else None
                else:
                    pairs.append((x * down + y, target[0] * down + target[1]))
        if not flatten:
            return lax.ppermute(part, axes, pairs)
        flat = part.reshape(-1)
        return lax.ppermute(flat, axes, pairs).reshape(part.shape)

    top, bottom = (value[..., :width, :], value[..., rows - width :, :])
    above = shift(bottom, "gy", 0, 1, flatten=False)
    below = shift(top, "gy", 0, -1, flatten=False)
    tall = jnp.concatenate([value, below, above], axis=-2)
    west = shift(tall[..., cols - width :], "gx", 1, 0)
    east = shift(tall[..., :width], "gx", -1, 0)
    return above, below, west, east


def forecast_kernel(cor_ref, x_ref, up_ref, down_ref, west_ref, east_ref, o_ref, ring, east_pad, west_pad, *, steps):
    rows, cols = (x_ref.shape[-2], x_ref.shape[-1])
    R, C = cor_ref.shape
    width = up_ref.shape[-2]
    spare = C - cols

    @pl.when(pl.program_id(0) == 0)
    def _():
        ring[...] = jnp.zeros_like(ring)
        east_pad[...] = jnp.zeros_like(east_pad)
        west_pad[...] = jnp.zeros_like(west_pad)

    for k in range(3):
        ring[k, :rows, :cols] = x_ref[0, k]
        ring[k, rows : rows + width, :cols] = down_ref[0, k]
        ring[k, rows + width :, :cols] = up_ref[0, k]
        east_pad[:, :width] = east_ref[0, k]
        west_pad[:, :width] = west_ref[0, k]
        ring[k, :, cols:] = east_pad[...] + pltpu.roll(west_pad[...], spare - width, 1)

    f = cor_ref[...]
    third = 1.0 / 12.0

    def dx(v):
        n_ = v.shape[1]
        g = pltpu.roll(v, n_ - 1, 1) - pltpu.roll(v, 1, 1)
        w = pltpu.roll(v, n_ - 2, 1) - pltpu.roll(v, 2, 1)
        return (8.0 * g - w) * third

    def dy(v):
        n_ = v.shape[0]
        g = pltpu.roll(v, n_ - 1, 0) - pltpu.roll(v, 1, 0)
        w = pltpu.roll(v, n_ - 2, 0) - pltpu.roll(v, 2, 0)
        return (8.0 * g - w) * third

    def shrink(v, margin, keep):
        size = v.shape[0]
        cut = margin - keep
        line = lax.broadcasted_iota(jnp.int32, v.shape, 0)
        moved = jnp.where(line < rows + keep, v, pltpu.roll(v, size - 2 * cut, 0))
        return moved[: size - 2 * cut]

    def tend(h, e, n):
        depth = 4.0 + h
        ch = -(dx(depth * e) + dy(depth * n))
        ce = -(e * dx(e) + n * dy(e)) + f * n - dx(h)
        cn = -(e * dx(n) + n * dy(n)) - f * e - dy(h)
        return ch, ce, cn

    s = (ring[0], ring[1], ring[2])
    margin = (R - rows) // 2
    for step in range(steps):
        keep = 4 * (steps - step)
        if keep < margin and (rows + 2 * keep) % 8 == 0:
            s = tuple(shrink(v, margin, keep) for v in s)
            f = shrink(f, margin, keep)
            margin = keep
        first = tend(*s)
        mid = tuple(a + 0.1 * b for a, b in zip(s, first))
        second = tend(*mid)
        s = tuple(a + 0.05 * (b + c) for a, b, c in zip(s, first, second))
    for k in range(3):
        o_ref[0, k] = s[k][:rows, :cols]


def forecast(cor, value, above, below, west, east, steps):
    S, F, rows, cols = value.shape
    R, C = cor.shape
    width = above.shape[-2]
    return pl.pallas_call(
        functools.partial(forecast_kernel, steps=steps),
        out_shape=jax.ShapeDtypeStruct((S, F, rows, cols), jnp.float32),
        grid=(S,),
        in_specs=[
            pl.BlockSpec((R, C), lambda i: (0, 0)),
            pl.BlockSpec((1, F, rows, cols), lambda i: (i, 0, 0, 0)),
            pl.BlockSpec((1, F, width, cols), lambda i: (i, 0, 0, 0)),
            pl.BlockSpec((1, F, width, cols), lambda i: (i, 0, 0, 0)),
            pl.BlockSpec((1, F, R, width), lambda i: (i, 0, 0, 0)),
            pl.BlockSpec((1, F, R, width), lambda i: (i, 0, 0, 0)),
        ],
        out_specs=pl.BlockSpec((1, F, rows, cols), lambda i: (i, 0, 0, 0)),
        scratch_shapes=[
            pltpu.VMEM((F, R, C), jnp.float32),
            pltpu.VMEM((R, C - cols), jnp.float32),
            pltpu.VMEM((R, C - cols), jnp.float32),
        ],
        cost_estimate=pl.CostEstimate(
            flops=S * F * R * C * 300 * steps, transcendentals=0, bytes_accessed=4 * S * F * (R * C + rows * cols)
        ),
    )(cor, value, above, below, west, east)


def body(control, perts):
    tile_rows, tile_column_count = (control.shape[1], control.shape[2])
    grid_rows = tile_rows * lax.axis_size("gy")
    grid_cols = tile_column_count * lax.axis_size("gx")
    first_row = lax.axis_index("gy") * tile_rows
    margin = 4 * STEPS
    lanes = 128 * (-(-(tile_column_count + 2 * margin) // 128))
    ring_rows = tile_rows + 2 * margin
    offsets = jnp.arange(ring_rows, dtype=jnp.int32)
    offsets = jnp.where(offsets < tile_rows + margin, offsets, offsets - ring_rows)
    rows = ((first_row + offsets) % grid_rows).astype(jnp.float32)
    coriolis = coriolis_mid * (1.0 + 0.5 * jnp.sin(two_pi * rows / float(grid_rows)))
    coriolis = jnp.broadcast_to(coriolis[:, None], (ring_rows, lanes))

    states = jnp.concatenate([control[None], control[None] + perts], 0)
    above, below, west, east = ring_halo(states, margin, lanes)
    current = forecast(coriolis, states, above, below, west, east, STEPS)
    bred = current[1:] - current[0:1]
    flat = bred.reshape(MEMBERS, -1)
    local_gram = jnp.dot(flat, flat.T, precision=lax.Precision.HIGH)
    gram = local_gram
    for axis in ("gx", "gy"):
        count = lax.axis_size(axis)
        if count & (count - 1):
            gram = lax.psum(gram, axis)
            continue
        stride = 1
        while stride < count:
            pairs = [(i, i ^ stride) for i in range(count)]
            gram = gram + lax.ppermute(gram, axis, pairs)
            stride *= 2
    lower = jnp.linalg.cholesky(gram)
    solved = jax.scipy.linalg.solve_triangular(lower, flat, lower=True)
    domain_length = 3 * grid_rows * grid_cols
    basis = (math.sqrt(domain_length) * solved).reshape(perts.shape)
    rfactor = lower.T / math.sqrt(domain_length)
    return (basis, rfactor)


def solution(mesh):
    in_specs = (P(None, "gy", "gx"), P(None, None, "gy", "gx"))
    out_specs = (P(None, None, "gy", "gx"), P())
    return jax.shard_map(body, mesh=mesh, in_specs=in_specs, out_specs=out_specs, check_vma=False)
```

```python
import functools
import math

import jax
import jax.numpy as jnp
from jax import lax
from jax.experimental import pallas as pl
from jax.experimental.pallas import tpu as pltpu
from jax.sharding import PartitionSpec as P

MEMBERS = 16
STEPS = 2


mean_depth = 4.0
gravity = 1.0
coriolis_mid = 0.5
time_step = 0.1
two_pi = 2.0 * math.pi


def ring_halo(value, width, lanes):
    rows, cols = (value.shape[-2], value.shape[-1])
    across, down = (lax.axis_size("gx"), lax.axis_size("gy"))

    def shift(part, axes, dx, dy, flatten=True):
        pairs = []
        for x in range(across):
            for y in range(down):
                target = ((x + dx) % across, (y + dy) % down)
                if axes == "gx":
                    pairs.append((x, target[0])) if y == 0 else None
                elif axes == "gy":
                    pairs.append((y, target[1])) if x == 0 else None
                else:
                    pairs.append((x * down + y, target[0] * down + target[1]))
        if not flatten:
            return lax.ppermute(part, axes, pairs)
        flat = part.reshape(-1)
        return lax.ppermute(flat, axes, pairs).reshape(part.shape)

    top, bottom = (value[..., :width, :], value[..., rows - width :, :])
    above = shift(bottom, "gy", 0, 1, flatten=False)
    below = shift(top, "gy", 0, -1, flatten=False)
    tall = jnp.concatenate([value, below, above], axis=-2)
    west = shift(tall[..., cols - width :], "gx", 1, 0)
    east = shift(tall[..., :width], "gx", -1, 0)
    return above, below, west, east


def forecast_kernel(cor_ref, x_ref, up_ref, down_ref, west_ref, east_ref, o_ref, ring, east_pad, west_pad, *, steps):
    rows, cols = (x_ref.shape[-2], x_ref.shape[-1])
    R, C = cor_ref.shape
    width = up_ref.shape[-2]
    spare = C - cols

    @pl.when(pl.program_id(0) == 0)
    def _():
        ring[...] = jnp.zeros_like(ring)
        east_pad[...] = jnp.zeros_like(east_pad)
        west_pad[...] = jnp.zeros_like(west_pad)

    for k in range(3):
        ring[k, :rows, :cols] = x_ref[0, k]
        ring[k, rows : rows + width, :cols] = down_ref[0, k]
        ring[k, rows + width :, :cols] = up_ref[0, k]
        east_pad[:, :width] = east_ref[0, k]
        west_pad[:, :width] = west_ref[0, k]
        ring[k, :, cols:] = east_pad[...] + pltpu.roll(west_pad[...], spare - width, 1)

    f = cor_ref[...]
    third = 1.0 / 12.0

    def dx(v):
        n_ = v.shape[1]
        g = pltpu.roll(v, n_ - 1, 1) - pltpu.roll(v, 1, 1)
        w = pltpu.roll(v, n_ - 2, 1) - pltpu.roll(v, 2, 1)
        return (8.0 * g - w) * third

    def dy(v):
        n_ = v.shape[0]
        g = pltpu.roll(v, n_ - 1, 0) - pltpu.roll(v, 1, 0)
        w = pltpu.roll(v, n_ - 2, 0) - pltpu.roll(v, 2, 0)
        return (8.0 * g - w) * third

    def shrink(v, margin, keep):
        size = v.shape[0]
        cut = margin - keep
        line = lax.broadcasted_iota(jnp.int32, v.shape, 0)
        moved = jnp.where(line < rows + keep, v, pltpu.roll(v, size - 2 * cut, 0))
        return moved[: size - 2 * cut]

    def tend(h, e, n):
        depth = 4.0 + h
        ch = -(dx(depth * e) + dy(depth * n))
        ce = -(e * dx(e) + n * dy(e)) + f * n - dx(h)
        cn = -(e * dx(n) + n * dy(n)) - f * e - dy(h)
        return ch, ce, cn

    s = (ring[0], ring[1], ring[2])
    margin = (R - rows) // 2
    for step in range(steps):
        keep = 4 * (steps - step)
        if keep < margin and (rows + 2 * keep) % 8 == 0:
            s = tuple(shrink(v, margin, keep) for v in s)
            f = shrink(f, margin, keep)
            margin = keep
        first = tend(*s)
        mid = tuple(a + 0.1 * b for a, b in zip(s, first))
        second = tend(*mid)
        s = tuple(a + 0.05 * (b + c) for a, b, c in zip(s, first, second))
    for k in range(3):
        o_ref[0, k] = s[k][:rows, :cols]


def forecast(cor, value, above, below, west, east, steps):
    S, F, rows, cols = value.shape
    R, C = cor.shape
    width = above.shape[-2]
    return pl.pallas_call(
        functools.partial(forecast_kernel, steps=steps),
        out_shape=jax.ShapeDtypeStruct((S, F, rows, cols), jnp.float32),
        grid=(S,),
        in_specs=[
            pl.BlockSpec((R, C), lambda i: (0, 0)),
            pl.BlockSpec((1, F, rows, cols), lambda i: (i, 0, 0, 0)),
            pl.BlockSpec((1, F, width, cols), lambda i: (i, 0, 0, 0)),
            pl.BlockSpec((1, F, width, cols), lambda i: (i, 0, 0, 0)),
            pl.BlockSpec((1, F, R, width), lambda i: (i, 0, 0, 0)),
            pl.BlockSpec((1, F, R, width), lambda i: (i, 0, 0, 0)),
        ],
        out_specs=pl.BlockSpec((1, F, rows, cols), lambda i: (i, 0, 0, 0)),
        scratch_shapes=[
            pltpu.VMEM((F, R, C), jnp.float32),
            pltpu.VMEM((R, C - cols), jnp.float32),
            pltpu.VMEM((R, C - cols), jnp.float32),
        ],
        cost_estimate=pl.CostEstimate(
            flops=S * F * R * C * 300 * steps, transcendentals=0, bytes_accessed=4 * S * F * (R * C + rows * cols)
        ),
    )(cor, value, above, below, west, east)


def body(control, perts):
    tile_rows, tile_column_count = (control.shape[1], control.shape[2])
    grid_rows = tile_rows * lax.axis_size("gy")
    grid_cols = tile_column_count * lax.axis_size("gx")
    first_row = lax.axis_index("gy") * tile_rows
    margin = 4 * STEPS
    lanes = 128 * (-(-(tile_column_count + 2 * margin) // 128))
    ring_rows = tile_rows + 2 * margin
    offsets = jnp.arange(ring_rows, dtype=jnp.int32)
    offsets = jnp.where(offsets < tile_rows + margin, offsets, offsets - ring_rows)
    rows = ((first_row + offsets) % grid_rows).astype(jnp.float32)
    coriolis = coriolis_mid * (1.0 + 0.5 * jnp.sin(two_pi * rows / float(grid_rows)))
    coriolis = jnp.broadcast_to(coriolis[:, None], (ring_rows, lanes))

    states = jnp.concatenate([control[None], control[None] + perts], 0)
    above, below, west, east = ring_halo(states, margin, lanes)
    current = forecast(coriolis, states, above, below, west, east, STEPS)
    bred = current[1:] - current[0:1]
    flat = bred.reshape(MEMBERS, -1)
    local_gram = jnp.dot(flat, flat.T, precision=lax.Precision.HIGH)
    gram = local_gram
    for axis in ("gx", "gy"):
        count = lax.axis_size(axis)
        if count & (count - 1):
            gram = lax.psum(gram, axis)
            continue
        stride = 1
        while stride < count:
            pairs = [(i, i ^ stride) for i in range(count)]
            gram = gram + lax.ppermute(gram, axis, pairs)
            stride *= 2
    lower = jnp.linalg.cholesky(gram)
    inverse = jax.scipy.linalg.solve_triangular(lower, jnp.eye(flat.shape[0], dtype=flat.dtype), lower=True)
    solved = jnp.dot(inverse, flat, precision=lax.Precision.HIGH)
    domain_length = 3 * grid_rows * grid_cols
    basis = (math.sqrt(domain_length) * solved).reshape(perts.shape)
    rfactor = lower.T / math.sqrt(domain_length)
    return (basis, rfactor)


def solution(mesh):
    in_specs = (P(None, "gy", "gx"), P(None, None, "gy", "gx"))
    out_specs = (P(None, None, "gy", "gx"), P())
    return jax.shard_map(body, mesh=mesh, in_specs=in_specs, out_specs=out_specs, check_vma=False)
```

```python
import functools
import math

import jax
import jax.numpy as jnp
from jax import lax
from jax.experimental import pallas as pl
from jax.experimental.pallas import tpu as pltpu
from jax.sharding import PartitionSpec as P

MEMBERS = 16
STEPS = 2


mean_depth = 4.0
gravity = 1.0
coriolis_mid = 0.5
time_step = 0.1
two_pi = 2.0 * math.pi


def ring_halo(value, width, lanes):
    rows, cols = (value.shape[-2], value.shape[-1])
    across, down = (lax.axis_size("gx"), lax.axis_size("gy"))

    def shift(part, axes, dx, dy, flatten=True):
        pairs = []
        for x in range(across):
            for y in range(down):
                target = ((x + dx) % across, (y + dy) % down)
                if axes == "gx":
                    pairs.append((x, target[0])) if y == 0 else None
                elif axes == "gy":
                    pairs.append((y, target[1])) if x == 0 else None
                else:
                    pairs.append((x * down + y, target[0] * down + target[1]))
        if not flatten:
            return lax.ppermute(part, axes, pairs)
        flat = part.reshape(-1)
        return lax.ppermute(flat, axes, pairs).reshape(part.shape)

    top, bottom = (value[..., :width, :], value[..., rows - width :, :])
    above = shift(bottom, "gy", 0, 1, flatten=False)
    below = shift(top, "gy", 0, -1, flatten=False)
    tall = jnp.concatenate([value, below, above], axis=-2)
    west = shift(tall[..., cols - width :], "gx", 1, 0)
    east = shift(tall[..., :width], "gx", -1, 0)
    return above, below, west, east


def forecast_kernel(cor_ref, x_ref, up_ref, down_ref, west_ref, east_ref, o_ref, ring, east_pad, west_pad, *, steps):
    rows, cols = (x_ref.shape[-2], x_ref.shape[-1])
    R, C = cor_ref.shape
    width = up_ref.shape[-2]
    spare = C - cols

    @pl.when(pl.program_id(0) == 0)
    def _():
        ring[...] = jnp.zeros_like(ring)
        east_pad[...] = jnp.zeros_like(east_pad)
        west_pad[...] = jnp.zeros_like(west_pad)

    for k in range(3):
        ring[k, :rows, :cols] = x_ref[0, k]
        ring[k, rows : rows + width, :cols] = down_ref[0, k]
        ring[k, rows + width :, :cols] = up_ref[0, k]
        east_pad[:, :width] = east_ref[0, k]
        west_pad[:, :width] = west_ref[0, k]
        ring[k, :, cols:] = east_pad[...] + pltpu.roll(west_pad[...], spare - width, 1)

    f = cor_ref[...]
    third = 1.0 / 12.0

    def dx(v):
        n_ = v.shape[1]
        g = pltpu.roll(v, n_ - 1, 1) - pltpu.roll(v, 1, 1)
        w = pltpu.roll(v, n_ - 2, 1) - pltpu.roll(v, 2, 1)
        return (8.0 * g - w) * third

    def dy(v):
        n_ = v.shape[0]
        g = pltpu.roll(v, n_ - 1, 0) - pltpu.roll(v, 1, 0)
        w = pltpu.roll(v, n_ - 2, 0) - pltpu.roll(v, 2, 0)
        return (8.0 * g - w) * third

    def shrink(v, margin, keep):
        size = v.shape[0]
        cut = margin - keep
        line = lax.broadcasted_iota(jnp.int32, v.shape, 0)
        moved = jnp.where(line < rows + keep, v, pltpu.roll(v, size - 2 * cut, 0))
        return moved[: size - 2 * cut]

    def tend(h, e, n):
        depth = 4.0 + h
        ch = -(dx(depth * e) + dy(depth * n))
        ce = -(e * dx(e) + n * dy(e)) + f * n - dx(h)
        cn = -(e * dx(n) + n * dy(n)) - f * e - dy(h)
        return ch, ce, cn

    s = (ring[0], ring[1], ring[2])
    margin = (R - rows) // 2
    for step in range(steps):
        keep = 4 * (steps - step)
        if keep < margin and (rows + 2 * keep) % 8 == 0:
            s = tuple(shrink(v, margin, keep) for v in s)
            f = shrink(f, margin, keep)
            margin = keep
        first = tend(*s)
        mid = tuple(a + 0.1 * b for a, b in zip(s, first))
        second = tend(*mid)
        s = tuple(a + 0.05 * (b + c) for a, b, c in zip(s, first, second))
    for k in range(3):
        o_ref[0, k] = s[k][:rows, :cols]


def forecast(cor, value, above, below, west, east, steps):
    S, F, rows, cols = value.shape
    R, C = cor.shape
    width = above.shape[-2]
    return pl.pallas_call(
        functools.partial(forecast_kernel, steps=steps),
        out_shape=jax.ShapeDtypeStruct((S, F, rows, cols), jnp.float32),
        grid=(S,),
        in_specs=[
            pl.BlockSpec((R, C), lambda i: (0, 0)),
            pl.BlockSpec((1, F, rows, cols), lambda i: (i, 0, 0, 0)),
            pl.BlockSpec((1, F, width, cols), lambda i: (i, 0, 0, 0)),
            pl.BlockSpec((1, F, width, cols), lambda i: (i, 0, 0, 0)),
            pl.BlockSpec((1, F, R, width), lambda i: (i, 0, 0, 0)),
            pl.BlockSpec((1, F, R, width), lambda i: (i, 0, 0, 0)),
        ],
        out_specs=pl.BlockSpec((1, F, rows, cols), lambda i: (i, 0, 0, 0)),
        scratch_shapes=[
            pltpu.VMEM((F, R, C), jnp.float32),
            pltpu.VMEM((R, C - cols), jnp.float32),
            pltpu.VMEM((R, C - cols), jnp.float32),
        ],
        compiler_params=pltpu.CompilerParams(allow_input_fusion=[True] * 6),
        cost_estimate=pl.CostEstimate(
            flops=S * F * R * C * 300 * steps, transcendentals=0, bytes_accessed=4 * S * F * (R * C + rows * cols)
        ),
    )(cor, value, above, below, west, east)


def body(control, perts):
    tile_rows, tile_column_count = (control.shape[1], control.shape[2])
    grid_rows = tile_rows * lax.axis_size("gy")
    grid_cols = tile_column_count * lax.axis_size("gx")
    first_row = lax.axis_index("gy") * tile_rows
    margin = 4 * STEPS
    lanes = 128 * (-(-(tile_column_count + 2 * margin) // 128))
    ring_rows = tile_rows + 2 * margin
    offsets = jnp.arange(ring_rows, dtype=jnp.int32)
    offsets = jnp.where(offsets < tile_rows + margin, offsets, offsets - ring_rows)
    rows = ((first_row + offsets) % grid_rows).astype(jnp.float32)
    coriolis = coriolis_mid * (1.0 + 0.5 * jnp.sin(two_pi * rows / float(grid_rows)))
    coriolis = jnp.broadcast_to(coriolis[:, None], (ring_rows, lanes))

    states = jnp.concatenate([control[None], control[None] + perts], 0)
    above, below, west, east = ring_halo(states, margin, lanes)
    current = forecast(coriolis, states, above, below, west, east, STEPS)
    bred = current[1:] - current[0:1]
    flat = bred.reshape(MEMBERS, -1)
    local_gram = jnp.dot(flat, flat.T, precision=lax.Precision.HIGH)
    gram = local_gram
    for axis in ("gx", "gy"):
        count = lax.axis_size(axis)
        if count & (count - 1):
            gram = lax.psum(gram, axis)
            continue
        stride = 1
        while stride < count:
            pairs = [(i, i ^ stride) for i in range(count)]
            gram = gram + lax.ppermute(gram, axis, pairs)
            stride *= 2
    lower = jnp.linalg.cholesky(gram)
    inverse = jax.scipy.linalg.solve_triangular(lower, jnp.eye(flat.shape[0], dtype=flat.dtype), lower=True)
    solved = jnp.dot(inverse, flat, precision=lax.Precision.HIGH)
    domain_length = 3 * grid_rows * grid_cols
    basis = (math.sqrt(domain_length) * solved).reshape(perts.shape)
    rfactor = lower.T / math.sqrt(domain_length)
    return (basis, rfactor)


def solution(mesh):
    in_specs = (P(None, "gy", "gx"), P(None, None, "gy", "gx"))
    out_specs = (P(None, None, "gy", "gx"), P())
    return jax.shard_map(body, mesh=mesh, in_specs=in_specs, out_specs=out_specs, check_vma=False)
```

```python
import functools
import math

import jax
import jax.numpy as jnp
from jax import lax
from jax.experimental import pallas as pl
from jax.experimental.pallas import tpu as pltpu
from jax.sharding import PartitionSpec as P

MEMBERS = 16
STEPS = 2


mean_depth = 4.0
gravity = 1.0
coriolis_mid = 0.5
time_step = 0.1
two_pi = 2.0 * math.pi


def ring_halo(value, width, lanes):
    rows, cols = (value.shape[-2], value.shape[-1])
    across, down = (lax.axis_size("gx"), lax.axis_size("gy"))

    def shift(part, axes, dx, dy, flatten=True):
        pairs = []
        for x in range(across):
            for y in range(down):
                target = ((x + dx) % across, (y + dy) % down)
                if axes == "gx":
                    pairs.append((x, target[0])) if y == 0 else None
                elif axes == "gy":
                    pairs.append((y, target[1])) if x == 0 else None
                else:
                    pairs.append((x * down + y, target[0] * down + target[1]))
        if not flatten:
            return lax.ppermute(part, axes, pairs)
        flat = part.reshape(-1)
        return lax.ppermute(flat, axes, pairs).reshape(part.shape)

    top, bottom = (value[..., :width, :], value[..., rows - width :, :])
    above = shift(bottom, "gy", 0, 1, flatten=False)
    below = shift(top, "gy", 0, -1, flatten=False)
    tall = jnp.concatenate([value, below, above], axis=-2)
    west = shift(tall[..., cols - width :], "gx", 1, 0)
    east = shift(tall[..., :width], "gx", -1, 0)
    return above, below, west, east


def forecast_kernel(cor_ref, x_ref, up_ref, down_ref, west_ref, east_ref, o_ref, ring, east_pad, west_pad, *, steps):
    rows, cols = (x_ref.shape[-2], x_ref.shape[-1])
    R, C = cor_ref.shape
    width = up_ref.shape[-2]
    spare = C - cols

    @pl.when(pl.program_id(0) == 0)
    def _():
        ring[...] = jnp.zeros_like(ring)
        east_pad[...] = jnp.zeros_like(east_pad)
        west_pad[...] = jnp.zeros_like(west_pad)

    for k in range(3):
        ring[k, :rows, :cols] = x_ref[0, k]
        ring[k, rows : rows + width, :cols] = down_ref[0, k]
        ring[k, rows + width :, :cols] = up_ref[0, k]
        east_pad[:, :width] = east_ref[0, k]
        west_pad[:, :width] = west_ref[0, k]
        ring[k, :, cols:] = east_pad[...] + pltpu.roll(west_pad[...], spare - width, 1)

    f = cor_ref[...]
    third = 1.0 / 12.0

    def dx(v):
        n_ = v.shape[1]
        g = pltpu.roll(v, n_ - 1, 1) - pltpu.roll(v, 1, 1)
        w = pltpu.roll(v, n_ - 2, 1) - pltpu.roll(v, 2, 1)
        return (8.0 * g - w) * third

    def dy(v):
        n_ = v.shape[0]
        g = pltpu.roll(v, n_ - 1, 0) - pltpu.roll(v, 1, 0)
        w = pltpu.roll(v, n_ - 2, 0) - pltpu.roll(v, 2, 0)
        return (8.0 * g - w) * third

    def shrink(v, margin, keep):
        size = v.shape[0]
        cut = margin - keep
        line = lax.broadcasted_iota(jnp.int32, v.shape, 0)
        moved = jnp.where(line < rows + keep, v, pltpu.roll(v, size - 2 * cut, 0))
        return moved[: size - 2 * cut]

    def tend(h, e, n):
        depth = 4.0 + h
        ch = -(dx(depth * e) + dy(depth * n))
        ce = -(e * dx(e) + n * dy(e)) + f * n - dx(h)
        cn = -(e * dx(n) + n * dy(n)) - f * e - dy(h)
        return ch, ce, cn

    s = (ring[0], ring[1], ring[2])
    margin = (R - rows) // 2
    for step in range(steps):
        keep = 4 * (steps - step)
        if keep < margin and (rows + 2 * keep) % 8 == 0:
            s = tuple(shrink(v, margin, keep) for v in s)
            f = shrink(f, margin, keep)
            margin = keep
        first = tend(*s)
        mid = tuple(a + 0.1 * b for a, b in zip(s, first))
        second = tend(*mid)
        s = tuple(a + 0.05 * (b + c) for a, b, c in zip(s, first, second))
    for k in range(3):
        o_ref[0, k] = s[k][:rows, :cols]


def forecast(cor, value, above, below, west, east, steps):
    S, F, rows, cols = value.shape
    R, C = cor.shape
    width = above.shape[-2]
    return pl.pallas_call(
        functools.partial(forecast_kernel, steps=steps),
        out_shape=jax.ShapeDtypeStruct((S, F, rows, cols), jnp.float32),
        grid=(S,),
        in_specs=[
            pl.BlockSpec((R, C), lambda i: (0, 0)),
            pl.BlockSpec((1, F, rows, cols), lambda i: (i, 0, 0, 0)),
            pl.BlockSpec((1, F, width, cols), lambda i: (i, 0, 0, 0)),
            pl.BlockSpec((1, F, width, cols), lambda i: (i, 0, 0, 0)),
            pl.BlockSpec((1, F, R, width), lambda i: (i, 0, 0, 0)),
            pl.BlockSpec((1, F, R, width), lambda i: (i, 0, 0, 0)),
        ],
        out_specs=pl.BlockSpec((1, F, rows, cols), lambda i: (i, 0, 0, 0)),
        scratch_shapes=[
            pltpu.VMEM((F, R, C), jnp.float32),
            pltpu.VMEM((R, C - cols), jnp.float32),
            pltpu.VMEM((R, C - cols), jnp.float32),
        ],
        cost_estimate=pl.CostEstimate(
            flops=S * F * R * C * 300 * steps, transcendentals=0, bytes_accessed=4 * S * F * (R * C + rows * cols)
        ),
    )(cor, value, above, below, west, east)


def body(control, perts):
    tile_rows, tile_column_count = (control.shape[1], control.shape[2])
    grid_rows = tile_rows * lax.axis_size("gy")
    grid_cols = tile_column_count * lax.axis_size("gx")
    first_row = lax.axis_index("gy") * tile_rows
    margin = 4 * STEPS
    lanes = 128 * (-(-(tile_column_count + 2 * margin) // 128))
    ring_rows = tile_rows + 2 * margin
    offsets = jnp.arange(ring_rows, dtype=jnp.int32)
    offsets = jnp.where(offsets < tile_rows + margin, offsets, offsets - ring_rows)
    rows = ((first_row + offsets) % grid_rows).astype(jnp.float32)
    coriolis = coriolis_mid * (1.0 + 0.5 * jnp.sin(two_pi * rows / float(grid_rows)))
    coriolis = jnp.broadcast_to(coriolis[:, None], (ring_rows, lanes))

    states = jnp.concatenate([control[None], control[None] + perts], 0)
    above, below, west, east = ring_halo(states, margin, lanes)
    current = forecast(coriolis, states, above, below, west, east, STEPS)
    bred = current[1:] - current[0:1]
    flat = bred.reshape(MEMBERS, -1)
    local_gram = jnp.dot(flat, flat.T, precision=lax.Precision.HIGH)
    gram = local_gram
    for axis in ("gx", "gy"):
        count = lax.axis_size(axis)
        if count & (count - 1):
            gram = lax.psum(gram, axis)
            continue
        stride = 1
        while stride < count:
            pairs = [(i, i ^ stride) for i in range(count)]
            gram = gram + lax.ppermute(gram, axis, pairs)
            stride *= 2
    domain_length = 3 * grid_rows * grid_cols
    lower = jnp.linalg.cholesky(gram * (1.0 / domain_length))
    inverse = jax.scipy.linalg.solve_triangular(lower, jnp.eye(flat.shape[0], dtype=flat.dtype), lower=True)
    basis = jnp.dot(inverse, flat, precision=lax.Precision.HIGH).reshape(perts.shape)
    rfactor = lower.T
    return (basis, rfactor)


def solution(mesh):
    in_specs = (P(None, "gy", "gx"), P(None, None, "gy", "gx"))
    out_specs = (P(None, None, "gy", "gx"), P())
    return jax.shard_map(body, mesh=mesh, in_specs=in_specs, out_specs=out_specs, check_vma=False)
```

```python
import functools
import math

import jax
import jax.numpy as jnp
from jax import lax
from jax.experimental import pallas as pl
from jax.experimental.pallas import tpu as pltpu
from jax.sharding import PartitionSpec as P

MEMBERS = 16
STEPS = 2


mean_depth = 4.0
gravity = 1.0
coriolis_mid = 0.5
time_step = 0.1
two_pi = 2.0 * math.pi


def ring_halo(value, width, lanes):
    rows, cols = (value.shape[-2], value.shape[-1])
    across, down = (lax.axis_size("gx"), lax.axis_size("gy"))

    def shift(part, axes, dx, dy, flatten=True):
        pairs = []
        for x in range(across):
            for y in range(down):
                target = ((x + dx) % across, (y + dy) % down)
                if axes == "gx":
                    pairs.append((x, target[0])) if y == 0 else None
                elif axes == "gy":
                    pairs.append((y, target[1])) if x == 0 else None
                else:
                    pairs.append((x * down + y, target[0] * down + target[1]))
        if not flatten:
            return lax.ppermute(part, axes, pairs)
        flat = part.reshape(-1)
        return lax.ppermute(flat, axes, pairs).reshape(part.shape)

    top, bottom = (value[..., :width, :], value[..., rows - width :, :])
    above = shift(bottom, "gy", 0, 1, flatten=False)
    below = shift(top, "gy", 0, -1, flatten=False)
    tall = jnp.concatenate([value, below, above], axis=-2)
    west = shift(tall[..., cols - width :], "gx", 1, 0)
    east = shift(tall[..., :width], "gx", -1, 0)
    return above, below, west, east


def forecast_kernel(cor_ref, x_ref, up_ref, down_ref, west_ref, east_ref, o_ref, ring, east_pad, west_pad, *, steps):
    rows, cols = (x_ref.shape[-2], x_ref.shape[-1])
    R, C = cor_ref.shape
    width = up_ref.shape[-2]
    spare = C - cols

    @pl.when(pl.program_id(0) == 0)
    def _():
        ring[...] = jnp.zeros_like(ring)
        east_pad[...] = jnp.zeros_like(east_pad)
        west_pad[...] = jnp.zeros_like(west_pad)

    for k in range(3):
        ring[k, :rows, :cols] = x_ref[0, k]
        ring[k, rows : rows + width, :cols] = down_ref[0, k]
        ring[k, rows + width :, :cols] = up_ref[0, k]
        east_pad[:, :width] = east_ref[0, k]
        west_pad[:, :width] = west_ref[0, k]
        ring[k, :, cols:] = east_pad[...] + pltpu.roll(west_pad[...], spare - width, 1)

    f = cor_ref[...]
    third = 1.0 / 12.0

    def dx(v):
        n_ = v.shape[1]
        g = pltpu.roll(v, n_ - 1, 1) - pltpu.roll(v, 1, 1)
        w = pltpu.roll(v, n_ - 2, 1) - pltpu.roll(v, 2, 1)
        return (8.0 * g - w) * third

    def dy(v):
        n_ = v.shape[0]
        g = pltpu.roll(v, n_ - 1, 0) - pltpu.roll(v, 1, 0)
        w = pltpu.roll(v, n_ - 2, 0) - pltpu.roll(v, 2, 0)
        return (8.0 * g - w) * third

    def shrink(v, margin, keep):
        size = v.shape[0]
        cut = margin - keep
        line = lax.broadcasted_iota(jnp.int32, v.shape, 0)
        moved = jnp.where(line < rows + keep, v, pltpu.roll(v, size - 2 * cut, 0))
        return moved[: size - 2 * cut]

    def tend(h, e, n):
        depth = 4.0 + h
        ch = -(dx(depth * e) + dy(depth * n))
        ce = -(e * dx(e) + n * dy(e)) + f * n - dx(h)
        cn = -(e * dx(n) + n * dy(n)) - f * e - dy(h)
        return ch, ce, cn

    s = (ring[0], ring[1], ring[2])
    margin = (R - rows) // 2
    for step in range(steps):
        keep = 4 * (steps - step)
        if keep < margin and (rows + 2 * keep) % 8 == 0:
            s = tuple(shrink(v, margin, keep) for v in s)
            f = shrink(f, margin, keep)
            margin = keep
        first = tend(*s)
        mid = tuple(a + 0.1 * b for a, b in zip(s, first))
        second = tend(*mid)
        s = tuple(a + 0.05 * (b + c) for a, b, c in zip(s, first, second))
    for k in range(3):
        o_ref[0, k] = s[k][:rows, :cols]


def forecast(cor, value, above, below, west, east, steps):
    S, F, rows, cols = value.shape
    R, C = cor.shape
    width = above.shape[-2]
    return pl.pallas_call(
        functools.partial(forecast_kernel, steps=steps),
        out_shape=jax.ShapeDtypeStruct((S, F, rows, cols), jnp.float32),
        grid=(S,),
        in_specs=[
            pl.BlockSpec((R, C), lambda i: (0, 0)),
            pl.BlockSpec((1, F, rows, cols), lambda i: (i, 0, 0, 0)),
            pl.BlockSpec((1, F, width, cols), lambda i: (i, 0, 0, 0)),
            pl.BlockSpec((1, F, width, cols), lambda i: (i, 0, 0, 0)),
            pl.BlockSpec((1, F, R, width), lambda i: (i, 0, 0, 0)),
            pl.BlockSpec((1, F, R, width), lambda i: (i, 0, 0, 0)),
        ],
        out_specs=pl.BlockSpec((1, F, rows, cols), lambda i: (i, 0, 0, 0)),
        scratch_shapes=[
            pltpu.VMEM((F, R, C), jnp.float32),
            pltpu.VMEM((R, C - cols), jnp.float32),
            pltpu.VMEM((R, C - cols), jnp.float32),
        ],
        compiler_params=pltpu.CompilerParams(allow_input_fusion=[True] + [False] * 5),
        cost_estimate=pl.CostEstimate(
            flops=S * F * R * C * 300 * steps, transcendentals=0, bytes_accessed=4 * S * F * (R * C + rows * cols)
        ),
    )(cor, value, above, below, west, east)


def body(control, perts):
    tile_rows, tile_column_count = (control.shape[1], control.shape[2])
    grid_rows = tile_rows * lax.axis_size("gy")
    grid_cols = tile_column_count * lax.axis_size("gx")
    first_row = lax.axis_index("gy") * tile_rows
    margin = 4 * STEPS
    lanes = 128 * (-(-(tile_column_count + 2 * margin) // 128))
    ring_rows = tile_rows + 2 * margin
    offsets = jnp.arange(ring_rows, dtype=jnp.int32)
    offsets = jnp.where(offsets < tile_rows + margin, offsets, offsets - ring_rows)
    rows = ((first_row + offsets) % grid_rows).astype(jnp.float32)
    coriolis = coriolis_mid * (1.0 + 0.5 * jnp.sin(two_pi * rows / float(grid_rows)))
    coriolis = jnp.broadcast_to(coriolis[:, None], (ring_rows, lanes))

    states = jnp.concatenate([control[None], control[None] + perts], 0)
    above, below, west, east = ring_halo(states, margin, lanes)
    current = forecast(coriolis, states, above, below, west, east, STEPS)
    bred = current[1:] - current[0:1]
    flat = bred.reshape(MEMBERS, -1)
    local_gram = jnp.dot(flat, flat.T, precision=lax.Precision.HIGH)
    gram = local_gram
    for axis in ("gx", "gy"):
        count = lax.axis_size(axis)
        if count & (count - 1):
            gram = lax.psum(gram, axis)
            continue
        stride = 1
        while stride < count:
            pairs = [(i, i ^ stride) for i in range(count)]
            gram = gram + lax.ppermute(gram, axis, pairs)
            stride *= 2
    lower = jnp.linalg.cholesky(gram)
    inverse = jax.scipy.linalg.solve_triangular(lower, jnp.eye(flat.shape[0], dtype=flat.dtype), lower=True)
    solved = jnp.dot(inverse, flat, precision=lax.Precision.HIGH)
    domain_length = 3 * grid_rows * grid_cols
    basis = (math.sqrt(domain_length) * solved).reshape(perts.shape)
    rfactor = lower.T / math.sqrt(domain_length)
    return (basis, rfactor)


def solution(mesh):
    in_specs = (P(None, "gy", "gx"), P(None, None, "gy", "gx"))
    out_specs = (P(None, None, "gy", "gx"), P())
    return jax.shard_map(body, mesh=mesh, in_specs=in_specs, out_specs=out_specs, check_vma=False)
```
